32 devices in a mesh: section: 4 (over x, core), tile: 8 (over z, y).
Axes of the slice: x: 2, y: 2, z: 4, core: 2. Of those that a mesh axis runs over, the one named last changes fastest.
Arguments:
- saved_inputs: float32 [4, 1, 128, 128, 128], P('section', None, None, 'tile'), may hold values from -6 to 6
- out_grad: float32 [1, 128, 128, 128], P(None, 'section', 'tile'), may hold values from -6 to 6
- pointwise: float32 [4, 128, 128], P('section'), may hold values from -0.5 to 0.5
- kernels: float32 [4, 9, 128], P('section'), may hold values from -2 to 2
- shifts: float32 [4, 128], P('section'), may hold values from -3 to 3
- gains: float32 [4, 128], P('section'), may hold values from 0.25 to 1.75
- rows_per_tile: int32 [8], P('tile'), may hold values from 4 to 16, as said below
- seam_codes: int32 [8, 2], P('tile'), may hold values from 0 to 1, as said below
Outputs:
- input_grads: float32 [4, 1, 128, 128, 128], P('section', None, None, 'tile')
- pointwise_grads: float32 [4, 128, 128], P('section')
- kernel_grads: float32 [4, 9, 128], P('section')
- shift_grads: float32 [4, 128], P('section')
- gain_grads: float32 [4, 128], P('section')
The draws below stay inside these ranges and needn't reach their ends.
Inputs may be any that keep to these rules, and one draw needn't show every extreme that they name: `rows_per_tile`: every tile holds 4 or more rows and some tile holds exactly 16. seam_codes[t, 1] equals seam_codes[t + 1, 0], cyclically in t.
All inputs are finite; a program needn't handle non-finite values.
Results may differ from the reference program's by a relative error of at most 0.0003.
Values sent between devices are 32-bit elements; how exact they have to be, the bound alone decides.
No kernel may reach another device: no remote copies, remote signals or barrier semaphores. Data moves between devices by JAX's collectives and lax.ppermute only.
A program may use at most 64 MiB of HBM per device.

```python
import math
import jax
import jax.numpy as jnp
from jax import lax

C = 128
COLS = 128
TILE_ROW_SLOTS = 16
KERNEL_DILATION = 4
M = 1
SECTIONS = 4
BAND_TILES = 8
ROWS = 128


def draw_rows_per_tile(key, part):
    initial_key = jax.random.fold_in(key, 11)
    second_key = jax.random.fold_in(key, 12)
    row_counts = jax.random.randint(initial_key, (BAND_TILES,), KERNEL_DILATION, TILE_ROW_SLOTS + 1)
    fullest = jax.random.randint(second_key, (), 0, BAND_TILES)
    return jnp.where(jnp.arange(BAND_TILES) == fullest, TILE_ROW_SLOTS, row_counts).astype(jnp.int32)


def draw_seam_codes(key, part):
    base_key = jax.random.fold_in(key, 21)
    upper_codes = jax.random.randint(base_key, (BAND_TILES,), 0, 2)
    lower_codes = jnp.roll(upper_codes, 1)
    return jnp.stack([lower_codes, upper_codes], axis=-1).astype(jnp.int32)


def levels(rng, dims, shards, smallest, top_value):
    def one(axis_at, shards_of):
        draws = jax.random.uniform(jax.random.fold_in(jax.random.fold_in(rng, 6), axis_at), (shards_of,), jnp.float32, smallest / len(shards), top_value / len(shards))
        return jnp.repeat(jnp.exp(draws), dims[axis_at] // shards_of).reshape((-1,) + (1,) * (len(dims) - axis_at - 1))

    level = one(*shards[0])
    for cut in shards[1:]:
        level = level * one(*cut)
    return level


def normal_values(rng, shape, spread, reach, pieces=(), held_as=jnp.bfloat16):
    level = levels(rng, shape, pieces, -0.22, 0.18) if pieces else 1.0
    result = jax.random.normal(rng, shape, jnp.float32) * spread * level
    return jnp.minimum(jnp.maximum(result, -reach), reach).astype(held_as)


def setup_inputs(seed: int = 0) -> dict:
    splits = jax.random.split(jax.random.key(seed), 9)
    saved_inputs = normal_values(splits[0], (SECTIONS, M, C, ROWS, COLS), 1.0, 6.0, ((0, 4), (3, 8)), jnp.float32)
    out_grad = normal_values(splits[1], (M, C, ROWS, COLS), 1.0, 6.0, ((1, 4), (2, 8)), jnp.float32)
    pointwise = normal_values(splits[2], (SECTIONS, C, C), C ** -0.5, 0.5, ((0, 4),), jnp.float32)
    kernels = normal_values(splits[3], (SECTIONS, 9, C), 9 ** -0.5, 2.0, ((0, 4),), jnp.float32)
    shifts = normal_values(splits[4], (SECTIONS, C), 0.5, 3.0, ((0, 4),), jnp.float32)
    gains = jnp.clip(1.0 + 0.15 * jax.random.normal(splits[5], (SECTIONS, C), jnp.float32), 0.25, 1.75)
    rows_per_tile = draw_rows_per_tile(jax.random.fold_in(splits[8], 71), 0)
    seam_codes = draw_seam_codes(jax.random.fold_in(splits[8], 71), 0)
    return dict(saved_inputs=saved_inputs, out_grad=out_grad, pointwise=pointwise, kernels=kernels, shifts=shifts, gains=gains, rows_per_tile=rows_per_tile, seam_codes=seam_codes)


def flipped(tile_row_block, code_value):
    return jnp.where(code_value == 1, tile_row_block[..., ::-1], tile_row_block)

def depthwise(extended_block, kernel_taps, slot_capacity_rows):
    column_total = extended_block.shape[2]
    padded_block = jnp.pad(extended_block, ((0, 0), (0, 0), (KERNEL_DILATION, KERNEL_DILATION)))
    running = jnp.zeros((extended_block.shape[0], slot_capacity_rows, column_total), jnp.float32)
    for row_offset_tap in range(3):
        for column_offset_tap in range(3):
            kernel_window = padded_block[:, row_offset_tap * KERNEL_DILATION:row_offset_tap * KERNEL_DILATION + slot_capacity_rows, column_offset_tap * KERNEL_DILATION:column_offset_tap * KERNEL_DILATION + column_total]
            running = running + kernel_taps[3 * row_offset_tap + column_offset_tap][:, None, None] * kernel_window
    return running

def section_forward(own_block, from_prev, received_from_next, row_total, weight_matrix, kernel_taps, shift_vector, gain_vector):
    slot_capacity_rows = own_block.shape[1]
    row_keep = (lax.iota(jnp.int32, slot_capacity_rows) < row_total).astype(jnp.float32)[None, :, None]
    masked_block = own_block * row_keep
    extended_block = jnp.concatenate([from_prev, masked_block, jnp.zeros_like(from_prev)], axis=1)
    extended_block = lax.dynamic_update_slice(extended_block, received_from_next, (jnp.int32(0), (row_total + KERNEL_DILATION).astype(jnp.int32), jnp.int32(0)))
    activation = depthwise(extended_block, kernel_taps, slot_capacity_rows) + shift_vector[:, None, None]
    channel_mean = lax.optimization_barrier(jnp.mean(activation, axis=0, keepdims=True))
    centered = activation - channel_mean
    variance = lax.optimization_barrier(jnp.mean(centered * centered, axis=0, keepdims=True))
    normalized = centered * lax.rsqrt(variance + 1e-06) * gain_vector[:, None, None]
    hidden = jax.nn.gelu(normalized)
    mixing = jnp.einsum('oc,crw->orw', weight_matrix, hidden, precision=lax.Precision.HIGHEST)
    return (masked_block + mixing) * row_keep

def section_apply(tiles, rows_per_tile, seam_codes, weight_matrix, kernel_taps, shift_vector, gain_vector):
    row_keep = (lax.iota(jnp.int32, TILE_ROW_SLOTS)[None, :] < rows_per_tile[:, None]).astype(jnp.float32)[:, None, :, None]
    masked_block = tiles * row_keep
    leading_rows = masked_block[:, :, :KERNEL_DILATION, :]
    trailing_rows = jax.vmap(lambda tile_row_block, row_total: lax.dynamic_slice_in_dim(tile_row_block, (row_total - KERNEL_DILATION).astype(jnp.int32), KERNEL_DILATION, 1))(masked_block, rows_per_tile)
    received_from_next = jax.vmap(flipped)(jnp.roll(leading_rows, -1, axis=0), seam_codes[:, 1])
    from_prev = jax.vmap(flipped)(jnp.roll(trailing_rows, 1, axis=0), seam_codes[:, 0])
    return jax.vmap(section_forward, in_axes=(0, 0, 0, 0, None, None, None, None))(tiles, from_prev, received_from_next, rows_per_tile, weight_matrix, kernel_taps, shift_vector, gain_vector)

def to_tiles(field):
    return field.reshape(C, BAND_TILES, TILE_ROW_SLOTS, COLS).transpose(1, 0, 2, 3)

def from_tiles(tiles):
    return tiles.transpose(1, 0, 2, 3).reshape(C, ROWS, COLS)

def reference(saved_inputs, out_grad, pointwise, kernels, shifts, gains, rows_per_tile, seam_codes):
    grad_scale = 1.0 / math.sqrt(M * ROWS * COLS)
    weight_totals = [jnp.zeros((C, C), jnp.float32) for section_number in range(SECTIONS)]
    kernel_totals = [jnp.zeros((9, C), jnp.float32) for section_number in range(SECTIONS)]
    shift_totals = [jnp.zeros((C,), jnp.float32) for section_number in range(SECTIONS)]
    gain_totals = [jnp.zeros((C,), jnp.float32) for section_number in range(SECTIONS)]
    input_rows = [[None] * M for section_number in range(SECTIONS)]
    for micro_index in range(M):
        cotangent = to_tiles(out_grad[micro_index])
        skip_grad = jnp.zeros_like(cotangent)
        for section_number in reversed(range(SECTIONS)):
            if section_number == 0:
                cotangent = cotangent + skip_grad

            def apply_block(tiles, weight_matrix, kernel_taps, shift_vector, gain_vector):
                return section_apply(tiles, rows_per_tile, seam_codes, weight_matrix, kernel_taps, shift_vector, gain_vector)
            outputs, pull = jax.vjp(apply_block, to_tiles(saved_inputs[section_number, micro_index]), pointwise[section_number], kernels[section_number], shifts[section_number], gains[section_number])
            grad_input, grad_weight, grad_kernel, grad_shift, grad_gain = pull(cotangent)
            weight_totals[section_number] = weight_totals[section_number] + grad_weight * grad_scale
            kernel_totals[section_number] = kernel_totals[section_number] + grad_kernel * grad_scale
            shift_totals[section_number] = shift_totals[section_number] + grad_shift * grad_scale
            gain_totals[section_number] = gain_totals[section_number] + grad_gain * grad_scale
            input_rows[section_number][micro_index] = from_tiles(grad_input)
            if section_number == SECTIONS - 1:
                skip_grad = grad_input
            cotangent = grad_input
    input_grads = jnp.stack([jnp.stack(input_rows[section_number]) for section_number in range(SECTIONS)])
    return (input_grads, jnp.stack(weight_totals), jnp.stack(kernel_totals), jnp.stack(shift_totals), jnp.stack(gain_totals))
```

```python
import math

import jax
import jax.numpy as jnp
from jax import lax
from jax.sharding import PartitionSpec as P

KERNEL_DILATION = 4
AXES = ("section", "tile")


def flipped(tile_row_block, code_value):
    return jnp.where(code_value == 1, tile_row_block[..., ::-1], tile_row_block)


def depthwise(extended_block, kernel_taps, slot_capacity_rows):
    column_total = extended_block.shape[2]
    columns = lax.iota(jnp.int32, column_total)
    running = jnp.zeros((extended_block.shape[0], slot_capacity_rows, column_total), jnp.float32)
    for column_offset_tap in range(3):
        offset = (column_offset_tap - 1) * KERNEL_DILATION
        moved = jnp.roll(extended_block, -offset, axis=2)
        inside = jnp.logical_and(columns + offset >= 0, columns + offset < column_total)
        moved = jnp.where(inside[None, None, :], moved, 0.0)
        for row_offset_tap in range(3):
            kernel_window = moved[
                :,
                row_offset_tap * KERNEL_DILATION : row_offset_tap * KERNEL_DILATION
                + slot_capacity_rows,
                :,
            ]
            running = (
                running
                + kernel_taps[3 * row_offset_tap + column_offset_tap][:, None, None] * kernel_window
            )
    return running


def section_forward(
    own_block,
    from_prev,
    received_from_next,
    row_total,
    weight_matrix,
    kernel_taps,
    shift_vector,
    gain_vector,
):
    slot_capacity_rows = own_block.shape[1]
    row_keep = (lax.iota(jnp.int32, slot_capacity_rows) < row_total).astype(jnp.float32)[
        None, :, None
    ]
    masked_block = own_block * row_keep
    extended_block = jnp.concatenate([from_prev, masked_block, jnp.zeros_like(from_prev)], axis=1)
    extended_block = lax.dynamic_update_slice(
        extended_block,
        received_from_next,
        (jnp.int32(0), row_total + KERNEL_DILATION, jnp.int32(0)),
    )
    activation = (
        depthwise(extended_block, kernel_taps, slot_capacity_rows) + shift_vector[:, None, None]
    )
    channel_mean = jnp.mean(activation, axis=0, keepdims=True)
    centered = activation - channel_mean
    variance = jnp.mean(centered * centered, axis=0, keepdims=True)
    normalized = centered * lax.rsqrt(variance + 1e-06) * gain_vector[:, None, None]
    hidden = jax.nn.gelu(normalized)
    mixing = jnp.einsum("oc,crw->orw", weight_matrix, hidden, precision=lax.Precision.HIGHEST)
    return (masked_block + mixing) * row_keep


def permute(x, pairs):
    return lax.ppermute(x, AXES, pairs)


def block_grads(own_block, params, cotangent, row_total, lower_code, upper_code, tiles):
    weight_matrix, kernel_taps, shift_vector, gain_vector = params
    slot_capacity_rows = own_block.shape[1]
    forward_pairs = [(t, (t + 1) % tiles) for t in range(tiles)]
    backward_pairs = [((t + 1) % tiles, t) for t in range(tiles)]
    row_keep = (lax.iota(jnp.int32, slot_capacity_rows) < row_total).astype(jnp.float32)[
        None, :, None
    ]
    masked_block = own_block * row_keep
    leading_rows = masked_block[:, :KERNEL_DILATION, :]
    trailing_rows = lax.dynamic_slice_in_dim(
        masked_block, row_total - KERNEL_DILATION, KERNEL_DILATION, 1
    )
    from_prev = flipped(permute(trailing_rows, forward_pairs), lower_code)
    received_from_next = flipped(permute(leading_rows, backward_pairs), upper_code)

    def apply_block(block_in, prev_in, next_in, weight_in, kernel_in, shift_in, gain_in):
        return section_forward(
            block_in, prev_in, next_in, row_total, weight_in, kernel_in, shift_in, gain_in
        )

    _, pull = jax.vjp(
        apply_block,
        own_block,
        from_prev,
        received_from_next,
        weight_matrix,
        kernel_taps,
        shift_vector,
        gain_vector,
    )
    grad_own, grad_prev, grad_next, grad_weight, grad_kernel, grad_shift, grad_gain = pull(
        cotangent
    )
    from_next_tile = permute(flipped(grad_prev, lower_code), backward_pairs)
    from_prev_tile = permute(flipped(grad_next, upper_code), forward_pairs)
    upper_part = lax.dynamic_update_slice_in_dim(
        jnp.zeros_like(own_block), from_next_tile, row_total - KERNEL_DILATION, 1
    )
    lower_part = jnp.pad(
        from_prev_tile, ((0, 0), (0, slot_capacity_rows - KERNEL_DILATION), (0, 0))
    )
    input_grad = grad_own + upper_part + lower_part
    packed = jnp.concatenate(
        [grad_weight, grad_kernel, grad_shift[None], grad_gain[None]], axis=0
    )
    return input_grad, packed


def butterfly_sum(x, section, tiles):
    if tiles & (tiles - 1):
        return lax.psum(x, "tile")
    step = 1
    while step < tiles:
        pairs = [(section * tiles + t, section * tiles + (t ^ step)) for t in range(tiles)]
        x = x + permute(x, pairs)
        step *= 2
    return x


def on_device(saved_inputs, out_grad, pointwise, kernels, shifts, gains, rows_per_tile, seam_codes):
    sections = lax.axis_size("section")
    tiles = lax.axis_size("tile")
    section_index = lax.axis_index("section")
    row_total = rows_per_tile[0]
    lower_code = seam_codes[0, 0]
    upper_code = seam_codes[0, 1]
    micro_count = saved_inputs.shape[1]
    channels = saved_inputs.shape[2]
    slot_capacity_rows = saved_inputs.shape[3]
    column_total = saved_inputs.shape[4]
    grad_scale = 1.0 / math.sqrt(micro_count * slot_capacity_rows * tiles * column_total)

    def to_head(x, source):
        if source == 0:
            return x
        return permute(x, [(source * tiles + t, t) for t in range(tiles)])

    def from_head(x, target):
        return permute(x, [(t, target * tiles + t) for t in range(tiles)])

    own_params = jnp.concatenate([pointwise[0], kernels[0], shifts, gains], axis=0)
    block_params = []
    for block in range(sections):
        packed = to_head(own_params, block)
        block_params.append(
            (
                packed[:channels],
                packed[channels : channels + 9],
                packed[channels + 9],
                packed[channels + 10],
            )
        )

    grad_totals = [None] * sections
    input_rows = [[None] * micro_count for _ in range(sections)]
    for micro_index in range(micro_count):
        top = jnp.concatenate(
            [to_head(out_grad[micro_index], block) for block in range(sections)], axis=0
        )
        cotangent = top
        skip_grad = None
        for block in reversed(range(sections)):
            if block == 0:
                cotangent = cotangent + skip_grad
            own_block = to_head(saved_inputs[0, micro_index], block)
            input_grad, packed = block_grads(
                own_block,
                block_params[block],
                cotangent,
                row_total,
                lower_code,
                upper_code,
                tiles,
            )
            grad_totals[block] = (
                packed if grad_totals[block] is None else grad_totals[block] + packed
            )
            input_rows[block][micro_index] = input_grad
            if block == sections - 1:
                skip_grad = input_grad
            cotangent = input_grad

    input_grads = None
    reduced = None
    for block in range(sections):
        rows = jnp.stack(input_rows[block])
        totals = grad_totals[block] * grad_scale
        if block != 0:
            rows = from_head(rows, block)
            totals = from_head(totals, block)
        totals = butterfly_sum(totals, block, tiles)
        mine = section_index == block
        input_grads = rows if input_grads is None else jnp.where(mine, rows, input_grads)
        reduced = totals if reduced is None else jnp.where(mine, totals, reduced)

    return (
        input_grads[None],
        reduced[None, :channels],
        reduced[None, channels : channels + 9],
        reduced[channels + 9][None],
        reduced[channels + 10][None],
    )


def solution(mesh):
    in_specs = (
        P("section", None, None, "tile", None),
        P(None, "section", "tile", None),
        P("section", None, None),
        P("section", None, None),
        P("section", None),
        P("section", None),
        P("tile"),
        P("tile", None),
    )
    out_specs = (
        P("section", None, None, "tile", None),
        P("section", None, None),
        P("section", None, None),
        P("section", None),
        P("section", None),
    )
    return jax.shard_map(
        on_device, mesh=mesh, in_specs=in_specs, out_specs=out_specs, check_vma=False
    )
```

```python
import math

import jax
import jax.numpy as jnp
from jax import lax
from jax.sharding import PartitionSpec as P

KERNEL_DILATION = 4
AXES = ("section", "tile")


def flipped(tile_row_block, code_value):
    return jnp.where(code_value == 1, tile_row_block[..., ::-1], tile_row_block)


def depthwise(extended_block, kernel_taps, slot_capacity_rows):
    column_total = extended_block.shape[2]
    columns = lax.iota(jnp.int32, column_total)
    running = jnp.zeros((extended_block.shape[0], slot_capacity_rows, column_total), jnp.float32)
    for column_offset_tap in range(3):
        offset = (column_offset_tap - 1) * KERNEL_DILATION
        moved = jnp.roll(extended_block, -offset, axis=2)
        inside = jnp.logical_and(columns + offset >= 0, columns + offset < column_total)
        moved = jnp.where(inside[None, None, :], moved, 0.0)
        for row_offset_tap in range(3):
            kernel_window = moved[
                :,
                row_offset_tap * KERNEL_DILATION : row_offset_tap * KERNEL_DILATION
                + slot_capacity_rows,
                :,
            ]
            running = (
                running
                + kernel_taps[3 * row_offset_tap + column_offset_tap][:, None, None] * kernel_window
            )
    return running


def section_forward(
    own_block,
    from_prev,
    received_from_next,
    row_total,
    weight_matrix,
    kernel_taps,
    shift_vector,
    gain_vector,
):
    slot_capacity_rows = own_block.shape[1]
    row_keep = (lax.iota(jnp.int32, slot_capacity_rows) < row_total).astype(jnp.float32)[
        None, :, None
    ]
    masked_block = own_block * row_keep
    extended_block = jnp.concatenate([from_prev, masked_block, jnp.zeros_like(from_prev)], axis=1)
    extended_block = lax.dynamic_update_slice(
        extended_block,
        received_from_next,
        (jnp.int32(0), row_total + KERNEL_DILATION, jnp.int32(0)),
    )
    activation = (
        depthwise(extended_block, kernel_taps, slot_capacity_rows) + shift_vector[:, None, None]
    )
    channel_mean = jnp.mean(activation, axis=0, keepdims=True)
    centered = activation - channel_mean
    variance = jnp.mean(centered * centered, axis=0, keepdims=True)
    normalized = centered * lax.rsqrt(variance + 1e-06) * gain_vector[:, None, None]
    hidden = jax.nn.gelu(normalized)
    mixing = jnp.einsum("oc,crw->orw", weight_matrix, hidden, precision=lax.Precision.HIGHEST)
    return (masked_block + mixing) * row_keep


def permute(x, pairs):
    return lax.ppermute(x, AXES, pairs)


def pack_rows(pieces, slot_rows, column_total):
    flat = jnp.concatenate([piece.reshape(-1) for piece in pieces])
    slab = slot_rows * column_total
    flat = jnp.pad(flat, (0, (-flat.shape[0]) % slab))
    return flat.reshape(-1, slot_rows, column_total)


def unpack_rows(slabs, shapes):
    flat = slabs.reshape(-1)
    out = []
    start = 0
    for shape in shapes:
        size = math.prod(shape)
        out.append(flat[start : start + size].reshape(shape))
        start += size
    return out


def edge_rows(own_block, row_total, lower_code, upper_code, tiles, pairs_of):
    slot_capacity_rows = own_block.shape[1]
    row_keep = (lax.iota(jnp.int32, slot_capacity_rows) < row_total).astype(jnp.float32)[
        None, :, None
    ]
    masked_block = own_block * row_keep
    leading_rows = masked_block[:, :KERNEL_DILATION, :]
    trailing_rows = lax.dynamic_slice_in_dim(
        masked_block, row_total - KERNEL_DILATION, KERNEL_DILATION, 1
    )
    forward_pairs, backward_pairs = pairs_of
    from_prev = flipped(permute(trailing_rows, forward_pairs), lower_code)
    received_from_next = flipped(permute(leading_rows, backward_pairs), upper_code)
    return from_prev, received_from_next


def block_grads(own_block, from_prev, received_from_next, params, cotangent, row_total, codes, pairs_of):
    weight_matrix, kernel_taps, shift_vector, gain_vector = params
    slot_capacity_rows = own_block.shape[1]
    forward_pairs, backward_pairs = pairs_of

    def apply_block(block_in, prev_in, next_in, weight_in, kernel_in, shift_in, gain_in):
        return section_forward(
            block_in, prev_in, next_in, row_total, weight_in, kernel_in, shift_in, gain_in
        )

    _, pull = jax.vjp(
        apply_block,
        own_block,
        from_prev,
        received_from_next,
        weight_matrix,
        kernel_taps,
        shift_vector,
        gain_vector,
    )
    grad_own, grad_prev, grad_next, grad_weight, grad_kernel, grad_shift, grad_gain = pull(
        cotangent
    )
    rims = jnp.stack([grad_prev, grad_next])
    rims = jnp.where((codes == 1)[:, None, None, None], rims[..., ::-1], rims)
    from_next_tile = permute(rims[0], backward_pairs)
    from_prev_tile = permute(rims[1], forward_pairs)
    upper_part = lax.dynamic_update_slice_in_dim(
        jnp.zeros_like(own_block), from_next_tile, row_total - KERNEL_DILATION, 1
    )
    lower_part = jnp.pad(
        from_prev_tile, ((0, 0), (0, slot_capacity_rows - KERNEL_DILATION), (0, 0))
    )
    input_grad = grad_own + upper_part + lower_part
    return input_grad, (grad_weight, grad_kernel, grad_shift, grad_gain)


def on_device(saved_inputs, out_grad, pointwise, kernels, shifts, gains, rows_per_tile, seam_codes):
    sections = lax.axis_size("section")
    tiles = lax.axis_size("tile")
    section_index = lax.axis_index("section")
    row_total = rows_per_tile[0]
    codes = seam_codes[0]
    lower_code = codes[0]
    upper_code = codes[1]
    micro_count = saved_inputs.shape[1]
    channels = saved_inputs.shape[2]
    slot_capacity_rows = saved_inputs.shape[3]
    column_total = saved_inputs.shape[4]
    grad_scale = 1.0 / math.sqrt(micro_count * slot_capacity_rows * tiles * column_total)
    og_channels = out_grad.shape[1]

    every_section = (
        [(s * tiles + t, s * tiles + (t + 1) % tiles) for s in range(sections) for t in range(tiles)],
        [(s * tiles + (t + 1) % tiles, s * tiles + t) for s in range(sections) for t in range(tiles)],
    )
    head_only = (
        [(t, (t + 1) % tiles) for t in range(tiles)],
        [((t + 1) % tiles, t) for t in range(tiles)],
    )
    param_shapes = [pointwise.shape[1:], kernels.shape[1:], shifts.shape[1:], gains.shape[1:]]
    halo_shape = (channels, KERNEL_DILATION, column_total)

    def to_head(x, source):
        if source == 0:
            return x
        return permute(x, [(source * tiles + t, t) for t in range(tiles)])

    def from_head(x, target):
        return permute(x, [(t, target * tiles + t) for t in range(tiles)])

    grad_parts = [None] * sections
    input_rows = [[None] * micro_count for _ in range(sections)]
    for micro_index in range(micro_count):
        own_block = saved_inputs[0, micro_index]
        from_prev, received_from_next = edge_rows(
            own_block, row_total, lower_code, upper_code, tiles, every_section
        )
        small = pack_rows(
            [from_prev, received_from_next, pointwise[0], kernels[0], shifts[0], gains[0]],
            slot_capacity_rows,
            column_total,
        )
        packed = jnp.concatenate([own_block, out_grad[micro_index], small], axis=0)
        block_data = []
        top_parts = []
        for block in range(sections):
            got = to_head(packed, block)
            pieces = unpack_rows(
                got[channels + og_channels :], [halo_shape, halo_shape] + param_shapes
            )
            block_data.append((got[:channels], pieces[0], pieces[1], tuple(pieces[2:])))
            top_parts.append(got[channels : channels + og_channels])
        cotangent = jnp.concatenate(top_parts, axis=0)
        skip_grad = None
        for block in reversed(range(sections)):
            if block == 0:
                cotangent = cotangent + skip_grad
            block_in, prev_in, next_in, params = block_data[block]
            input_grad, grads = block_grads(
                block_in, prev_in, next_in, params, cotangent, row_total, codes, head_only
            )
            grad_parts[block] = (
                grads
                if grad_parts[block] is None
                else tuple(a + b for a, b in zip(grad_parts[block], grads))
            )
            input_rows[block][micro_index] = input_grad
            if block == sections - 1:
                skip_grad = input_grad
            cotangent = input_grad

    input_grads = None
    partial = None
    for block in range(sections):
        rows = jnp.stack(input_rows[block])
        small = pack_rows(grad_parts[block], slot_capacity_rows, column_total)
        if block != 0:
            both = from_head(jnp.concatenate([rows.reshape(-1, slot_capacity_rows, column_total), small], axis=0), block)
            rows = both[: micro_count * channels].reshape(rows.shape)
            small = both[micro_count * channels :]
        mine = section_index == block
        input_grads = rows if input_grads is None else jnp.where(mine, rows, input_grads)
        partial = small if partial is None else jnp.where(mine, small, partial)

    partial = partial * grad_scale
    if tiles & (tiles - 1):
        partial = lax.psum(partial, "tile")
    else:
        step = 1
        while step < tiles:
            pairs = [
                (s * tiles + t, s * tiles + (t ^ step)) for s in range(sections) for t in range(tiles)
            ]
            partial = partial + permute(partial, pairs)
            step *= 2
    grad_weight, grad_kernel, grad_shift, grad_gain = unpack_rows(partial, param_shapes)
    return (
        input_grads[None],
        grad_weight[None],
        grad_kernel[None],
        grad_shift[None],
        grad_gain[None],
    )


def solution(mesh):
    in_specs = (
        P("section", None, None, "tile", None),
        P(None, "section", "tile", None),
        P("section", None, None),
        P("section", None, None),
        P("section", None),
        P("section", None),
        P("tile"),
        P("tile", None),
    )
    out_specs = (
        P("section", None, None, "tile", None),
        P("section", None, None),
        P("section", None, None),
        P("section", None),
        P("section", None),
    )
    return jax.shard_map(
        on_device, mesh=mesh, in_specs=in_specs, out_specs=out_specs, check_vma=False
    )
```

```python
import math

import jax
import jax.numpy as jnp
from jax import lax
from jax.sharding import PartitionSpec as P

KERNEL_DILATION = 4
AXES = ("section", "tile")


def flipped(tile_row_block, code_value):
    return jnp.where(code_value == 1, tile_row_block[..., ::-1], tile_row_block)


def depthwise(extended_block, kernel_taps, slot_capacity_rows):
    column_total = extended_block.shape[2]
    columns = lax.iota(jnp.int32, column_total)
    running = jnp.zeros((extended_block.shape[0], slot_capacity_rows, column_total), jnp.float32)
    for column_offset_tap in range(3):
        offset = (column_offset_tap - 1) * KERNEL_DILATION
        moved = jnp.roll(extended_block, -offset, axis=2)
        inside = jnp.logical_and(columns + offset >= 0, columns + offset < column_total)
        moved = jnp.where(inside[None, None, :], moved, 0.0)
        for row_offset_tap in range(3):
            kernel_window = moved[
                :,
                row_offset_tap * KERNEL_DILATION : row_offset_tap * KERNEL_DILATION
                + slot_capacity_rows,
                :,
            ]
            running = (
                running
                + kernel_taps[3 * row_offset_tap + column_offset_tap][:, None, None] * kernel_window
            )
    return running


def section_forward(
    own_block,
    from_prev,
    received_from_next,
    row_total,
    weight_matrix,
    kernel_taps,
    shift_vector,
    gain_vector,
):
    slot_capacity_rows = own_block.shape[1]
    row_keep = (lax.iota(jnp.int32, slot_capacity_rows) < row_total).astype(jnp.float32)[
        None, :, None
    ]
    masked_block = own_block * row_keep
    extended_block = jnp.concatenate([from_prev, masked_block, jnp.zeros_like(from_prev)], axis=1)
    extended_block = lax.dynamic_update_slice(
        extended_block,
        received_from_next,
        (jnp.int32(0), row_total + KERNEL_DILATION, jnp.int32(0)),
    )
    activation = (
        depthwise(extended_block, kernel_taps, slot_capacity_rows) + shift_vector[:, None, None]
    )
    channel_mean = jnp.mean(activation, axis=0, keepdims=True)
    centered = activation - channel_mean
    variance = jnp.mean(centered * centered, axis=0, keepdims=True)
    normalized = centered * lax.rsqrt(variance + 1e-06) * gain_vector[:, None, None]
    hidden = jax.nn.gelu(normalized)
    mixing = jnp.einsum("oc,crw->orw", weight_matrix, hidden, precision=lax.Precision.HIGHEST)
    return (masked_block + mixing) * row_keep


def permute(x, pairs):
    return lax.ppermute(x, AXES, pairs)


def pack_rows(pieces, slot_rows, column_total):
    flat = jnp.concatenate([piece.reshape(-1) for piece in pieces])
    slab = slot_rows * column_total
    flat = jnp.pad(flat, (0, (-flat.shape[0]) % slab))
    return flat.reshape(-1, slot_rows, column_total)


def unpack_rows(slabs, shapes):
    flat = slabs.reshape(-1)
    out = []
    start = 0
    for shape in shapes:
        size = math.prod(shape)
        out.append(flat[start : start + size].reshape(shape))
        start += size
    return out


def edge_rows(own_block, row_total, lower_code, upper_code, tiles, pairs_of):
    slot_capacity_rows = own_block.shape[1]
    row_keep = (lax.iota(jnp.int32, slot_capacity_rows) < row_total).astype(jnp.float32)[
        None, :, None
    ]
    masked_block = own_block * row_keep
    leading_rows = masked_block[:, :KERNEL_DILATION, :]
    trailing_rows = lax.dynamic_slice_in_dim(
        masked_block, row_total - KERNEL_DILATION, KERNEL_DILATION, 1
    )
    forward_pairs, backward_pairs = pairs_of
    from_prev = flipped(permute(trailing_rows, forward_pairs), lower_code)
    received_from_next = flipped(permute(leading_rows, backward_pairs), upper_code)
    return from_prev, received_from_next


def on_device(saved_inputs, out_grad, pointwise, kernels, shifts, gains, rows_per_tile, seam_codes):
    sections = lax.axis_size("section")
    tiles = lax.axis_size("tile")
    section_index = lax.axis_index("section")
    row_total = rows_per_tile[0]
    codes = seam_codes[0]
    lower_code = codes[0]
    upper_code = codes[1]
    micro_count = saved_inputs.shape[1]
    channels = saved_inputs.shape[2]
    slot_capacity_rows = saved_inputs.shape[3]
    column_total = saved_inputs.shape[4]
    grad_scale = 1.0 / math.sqrt(micro_count * slot_capacity_rows * tiles * column_total)
    every_section = (
        [(s * tiles + t, s * tiles + (t + 1) % tiles) for s in range(sections) for t in range(tiles)],
        [(s * tiles + (t + 1) % tiles, s * tiles + t) for s in range(sections) for t in range(tiles)],
    )
    params = (pointwise[0], kernels[0], shifts[0], gains[0])
    param_shapes = [pointwise.shape[1:], kernels.shape[1:], shifts.shape[1:], gains.shape[1:]]
    whole_top = lax.all_gather(out_grad, "section", axis=1, tiled=True)

    def apply_block(block_in, prev_in, next_in, weight_in, kernel_in, shift_in, gain_in):
        return section_forward(
            block_in, prev_in, next_in, row_total, weight_in, kernel_in, shift_in, gain_in
        )

    pulls = []
    for micro_index in range(micro_count):
        own_block = saved_inputs[0, micro_index]
        from_prev, received_from_next = edge_rows(
            own_block, row_total, lower_code, upper_code, tiles, every_section
        )
        _, pull = jax.vjp(apply_block, own_block, from_prev, received_from_next, *params)
        pulls.append(pull)

    def pull_at(slot_index, cotangent):
        if micro_count == 1:
            return pulls[0](cotangent)
        outs = [pull(cotangent) for pull in pulls]
        return tuple(
            sum(jnp.where(slot_index == m, o[k], 0.0) for m, o in enumerate(outs))
            for k in range(len(outs[0]))
        )

    forward_pairs, backward_pairs = every_section
    incoming = jnp.zeros((channels, slot_capacity_rows, column_total), jnp.float32)
    skip_store = jnp.zeros((micro_count, channels, slot_capacity_rows, column_total), jnp.float32)
    input_grads = jnp.zeros((micro_count, channels, slot_capacity_rows, column_total), jnp.float32)
    grad_totals = tuple(jnp.zeros(shape, jnp.float32) for shape in param_shapes)
    step_total = micro_count + sections - 1
    is_last = section_index == sections - 1
    for step_number in range(step_total):
        position = step_number - (sections - 1 - section_index)
        live_step = jnp.logical_and(position >= 0, position < micro_count)
        slot_index = jnp.clip(position, 0, micro_count - 1)
        top_grad = lax.dynamic_index_in_dim(whole_top, slot_index, 0, keepdims=False)
        grad_out = jnp.where(is_last, top_grad, incoming)
        if step_number >= sections - 1:
            carried = lax.dynamic_index_in_dim(skip_store, slot_index, 0, keepdims=False)
            grad_out = grad_out + jnp.where(section_index == 0, carried, 0.0)
        grad_own, grad_prev, grad_next, *grads = pull_at(slot_index, grad_out)
        rims = jnp.stack([grad_prev, grad_next])
        rims = jnp.where((codes == 1)[:, None, None, None], rims[..., ::-1], rims)
        from_next_tile = permute(rims[0], backward_pairs)
        from_prev_tile = permute(rims[1], forward_pairs)
        upper_part = lax.dynamic_update_slice_in_dim(
            jnp.zeros_like(grad_own), from_next_tile, row_total - KERNEL_DILATION, 1
        )
        lower_part = jnp.pad(
            from_prev_tile, ((0, 0), (0, slot_capacity_rows - KERNEL_DILATION), (0, 0))
        )
        input_grad = grad_own + upper_part + lower_part
        grad_totals = tuple(
            jnp.where(live_step, running + term, running) for running, term in zip(grad_totals, grads)
        )
        input_grads = jnp.where(
            live_step,
            lax.dynamic_update_index_in_dim(input_grads, input_grad, slot_index, 0),
            input_grads,
        )
        if step_number + 1 < step_total:
            incoming = from_behind(input_grad, "section", -1)
        if step_number == micro_count - 1:
            skip_store = from_behind(input_grads, "section", 1 - sections)

    partial = pack_rows(grad_totals, slot_capacity_rows, column_total) * grad_scale
    if tiles & (tiles - 1):
        partial = lax.psum(partial, "tile")
    else:
        step = 1
        while step < tiles:
            pairs = [
                (s * tiles + t, s * tiles + (t ^ step)) for s in range(sections) for t in range(tiles)
            ]
            partial = partial + permute(partial, pairs)
            step *= 2
    grad_weight, grad_kernel, grad_shift, grad_gain = unpack_rows(partial, param_shapes)
    return (
        input_grads[None],
        grad_weight[None],
        grad_kernel[None],
        grad_shift[None],
        grad_gain[None],
    )


def from_behind(block, axis, distance):
    devices = range(lax.axis_size(axis))
    route = [(i - distance, i) for i in devices if i - distance in devices]
    return lax.ppermute(block, axis, route)


def solution(mesh):
    in_specs = (
        P("section", None, None, "tile", None),
        P(None, "section", "tile", None),
        P("section", None, None),
        P("section", None, None),
        P("section", None),
        P("section", None),
        P("tile"),
        P("tile", None),
    )
    out_specs = (
        P("section", None, None, "tile", None),
        P("section", None, None),
        P("section", None, None),
        P("section", None),
        P("section", None),
    )
    return jax.shard_map(
        on_device, mesh=mesh, in_specs=in_specs, out_specs=out_specs, check_vma=False
    )
```

```python
import math

import jax
import jax.numpy as jnp
from jax import lax
from jax.sharding import PartitionSpec as P

KERNEL_DILATION = 4
AXES = ("section", "tile")


def flipped(tile_row_block, code_value):
    return jnp.where(code_value == 1, tile_row_block[..., ::-1], tile_row_block)


def depthwise(extended_block, kernel_taps, slot_capacity_rows):
    column_total = extended_block.shape[2]
    columns = lax.iota(jnp.int32, column_total)
    running = jnp.zeros((extended_block.shape[0], slot_capacity_rows, column_total), jnp.float32)
    for column_offset_tap in range(3):
        offset = (column_offset_tap - 1) * KERNEL_DILATION
        moved = jnp.roll(extended_block, -offset, axis=2)
        inside = jnp.logical_and(columns + offset >= 0, columns + offset < column_total)
        moved = jnp.where(inside[None, None, :], moved, 0.0)
        for row_offset_tap in range(3):
            kernel_window = moved[
                :,
                row_offset_tap * KERNEL_DILATION : row_offset_tap * KERNEL_DILATION
                + slot_capacity_rows,
                :,
            ]
            running = (
                running
                + kernel_taps[3 * row_offset_tap + column_offset_tap][:, None, None] * kernel_window
            )
    return running


def section_forward(
    own_block,
    from_prev,
    received_from_next,
    row_total,
    weight_matrix,
    kernel_taps,
    shift_vector,
    gain_vector,
):
    slot_capacity_rows = own_block.shape[1]
    row_keep = (lax.iota(jnp.int32, slot_capacity_rows) < row_total).astype(jnp.float32)[
        None, :, None
    ]
    masked_block = own_block * row_keep
    extended_block = jnp.concatenate([from_prev, masked_block, jnp.zeros_like(from_prev)], axis=1)
    extended_block = lax.dynamic_update_slice(
        extended_block,
        received_from_next,
        (jnp.int32(0), row_total + KERNEL_DILATION, jnp.int32(0)),
    )
    activation = (
        depthwise(extended_block, kernel_taps, slot_capacity_rows) + shift_vector[:, None, None]
    )
    channel_mean = jnp.mean(activation, axis=0, keepdims=True)
    centered = activation - channel_mean
    variance = jnp.mean(centered * centered, axis=0, keepdims=True)
    normalized = centered * lax.rsqrt(variance + 1e-06) * gain_vector[:, None, None]
    hidden = jax.nn.gelu(normalized)
    mixing = jnp.einsum("oc,crw->orw", weight_matrix, hidden, precision=lax.Precision.HIGHEST)
    return (masked_block + mixing) * row_keep


def permute(x, pairs):
    return lax.ppermute(x, AXES, pairs)


def pack_rows(pieces, slot_rows, column_total):
    flat = jnp.concatenate([piece.reshape(-1) for piece in pieces])
    slab = slot_rows * column_total
    flat = jnp.pad(flat, (0, (-flat.shape[0]) % slab))
    return flat.reshape(-1, slot_rows, column_total)


def unpack_rows(slabs, shapes):
    flat = slabs.reshape(-1)
    out = []
    start = 0
    for shape in shapes:
        size = math.prod(shape)
        out.append(flat[start : start + size].reshape(shape))
        start += size
    return out


def seam_matrices(codes, column_total):
    columns = lax.iota(jnp.int32, column_total)
    plain = (columns[:, None] == columns[None, :]).astype(jnp.float32)
    mirror = (columns[:, None] + columns[None, :] == column_total - 1).astype(jnp.float32)
    return jnp.where((codes == 1)[:, None, None], mirror[None], plain[None])


def seam_read(rims, matrices):
    return jnp.einsum("kcrw,kwv->kcrv", rims, matrices, precision=lax.Precision.HIGHEST)


def edge_rows(own_block, row_total, matrices, pairs_of):
    slot_capacity_rows = own_block.shape[1]
    row_keep = (lax.iota(jnp.int32, slot_capacity_rows) < row_total).astype(jnp.float32)[
        None, :, None
    ]
    masked_block = own_block * row_keep
    leading_rows = masked_block[:, :KERNEL_DILATION, :]
    trailing_rows = lax.dynamic_slice_in_dim(
        masked_block, row_total - KERNEL_DILATION, KERNEL_DILATION, 1
    )
    forward_pairs, backward_pairs = pairs_of
    rims = jnp.stack([permute(trailing_rows, forward_pairs), permute(leading_rows, backward_pairs)])
    rims = seam_read(rims, matrices)
    return rims[0], rims[1]


def on_device(saved_inputs, out_grad, pointwise, kernels, shifts, gains, rows_per_tile, seam_codes):
    sections = lax.axis_size("section")
    tiles = lax.axis_size("tile")
    section_index = lax.axis_index("section")
    row_total = rows_per_tile[0]
    codes = seam_codes[0]
    lower_code = codes[0]
    upper_code = codes[1]
    micro_count = saved_inputs.shape[1]
    channels = saved_inputs.shape[2]
    slot_capacity_rows = saved_inputs.shape[3]
    column_total = saved_inputs.shape[4]
    grad_scale = 1.0 / math.sqrt(micro_count * slot_capacity_rows * tiles * column_total)
    every_section = (
        [(s * tiles + t, s * tiles + (t + 1) % tiles) for s in range(sections) for t in range(tiles)],
        [(s * tiles + (t + 1) % tiles, s * tiles + t) for s in range(sections) for t in range(tiles)],
    )
    params = (pointwise[0], kernels[0], shifts[0], gains[0])
    param_shapes = [pointwise.shape[1:], kernels.shape[1:], shifts.shape[1:], gains.shape[1:]]
    whole_top = lax.all_gather(out_grad, "section", axis=1, tiled=True)
    matrices = seam_matrices(codes, column_total)

    def apply_block(block_in, prev_in, next_in, weight_in, kernel_in, shift_in, gain_in):
        return section_forward(
            block_in, prev_in, next_in, row_total, weight_in, kernel_in, shift_in, gain_in
        )

    pulls = []
    for micro_index in range(micro_count):
        own_block = saved_inputs[0, micro_index]
        from_prev, received_from_next = edge_rows(
            own_block, row_total, matrices, every_section
        )
        _, pull = jax.vjp(apply_block, own_block, from_prev, received_from_next, *params)
        pulls.append(pull)

    def pull_at(slot_index, cotangent):
        if micro_count == 1:
            return pulls[0](cotangent)
        outs = [pull(cotangent) for pull in pulls]
        return tuple(
            sum(jnp.where(slot_index == m, o[k], 0.0) for m, o in enumerate(outs))
            for k in range(len(outs[0]))
        )

    forward_pairs, backward_pairs = every_section
    incoming = jnp.zeros((channels, slot_capacity_rows, column_total), jnp.float32)
    skip_store = jnp.zeros((micro_count, channels, slot_capacity_rows, column_total), jnp.float32)
    input_grads = jnp.zeros((micro_count, channels, slot_capacity_rows, column_total), jnp.float32)
    grad_totals = tuple(jnp.zeros(shape, jnp.float32) for shape in param_shapes)
    step_total = micro_count + sections - 1
    is_last = section_index == sections - 1
    for step_number in range(step_total):
        position = step_number - (sections - 1 - section_index)
        live_step = jnp.logical_and(position >= 0, position < micro_count)
        slot_index = jnp.clip(position, 0, micro_count - 1)
        top_grad = lax.dynamic_index_in_dim(whole_top, slot_index, 0, keepdims=False)
        grad_out = jnp.where(is_last, top_grad, incoming)
        if step_number >= sections - 1:
            carried = lax.dynamic_index_in_dim(skip_store, slot_index, 0, keepdims=False)
            grad_out = grad_out + jnp.where(section_index == 0, carried, 0.0)
        grad_own, grad_prev, grad_next, *grads = pull_at(slot_index, grad_out)
        rims = jnp.stack([grad_prev, grad_next])
        rims = seam_read(rims, matrices)
        from_next_tile = permute(rims[0], backward_pairs)
        from_prev_tile = permute(rims[1], forward_pairs)
        upper_part = lax.dynamic_update_slice_in_dim(
            jnp.zeros_like(grad_own), from_next_tile, row_total - KERNEL_DILATION, 1
        )
        lower_part = jnp.pad(
            from_prev_tile, ((0, 0), (0, slot_capacity_rows - KERNEL_DILATION), (0, 0))
        )
        input_grad = grad_own + upper_part + lower_part
        grad_totals = tuple(
            jnp.where(live_step, running + term, running) for running, term in zip(grad_totals, grads)
        )
        input_grads = jnp.where(
            live_step,
            lax.dynamic_update_index_in_dim(input_grads, input_grad, slot_index, 0),
            input_grads,
        )
        if step_number + 1 < step_total:
            incoming = from_behind(input_grad, "section", -1)
        if step_number == micro_count - 1:
            skip_store = from_behind(input_grads, "section", 1 - sections)

    partial = pack_rows(grad_totals, slot_capacity_rows, column_total) * grad_scale
    if tiles & (tiles - 1):
        partial = lax.psum(partial, "tile")
    else:
        step = 1
        while step < tiles:
            pairs = [
                (s * tiles + t, s * tiles + (t ^ step)) for s in range(sections) for t in range(tiles)
            ]
            partial = partial + permute(partial, pairs)
            step *= 2
    grad_weight, grad_kernel, grad_shift, grad_gain = unpack_rows(partial, param_shapes)
    return (
        input_grads[None],
        grad_weight[None],
        grad_kernel[None],
        grad_shift[None],
        grad_gain[None],
    )


def from_behind(block, axis, distance):
    devices = range(lax.axis_size(axis))
    route = [(i - distance, i) for i in devices if i - distance in devices]
    return lax.ppermute(block, axis, route)


def solution(mesh):
    in_specs = (
        P("section", None, None, "tile", None),
        P(None, "section", "tile", None),
        P("section", None, None),
        P("section", None, None),
        P("section", None),
        P("section", None),
        P("tile"),
        P("tile", None),
    )
    out_specs = (
        P("section", None, None, "tile", None),
        P("section", None, None),
        P("section", None, None),
        P("section", None),
        P("section", None),
    )
    return jax.shard_map(
        on_device, mesh=mesh, in_specs=in_specs, out_specs=out_specs, check_vma=False
    )
```

```python
import math

import jax
import jax.numpy as jnp
from jax import lax
from jax.sharding import PartitionSpec as P

KERNEL_DILATION = 4
AXES = ("section", "tile")


def flipped(tile_row_block, code_value):
    return jnp.where(code_value == 1, tile_row_block[..., ::-1], tile_row_block)


def depthwise(extended_block, kernel_taps, slot_capacity_rows):
    column_total = extended_block.shape[2]
    columns = lax.iota(jnp.int32, column_total)
    running = jnp.zeros((extended_block.shape[0], slot_capacity_rows, column_total), jnp.float32)
    for column_offset_tap in range(3):
        offset = (column_offset_tap - 1) * KERNEL_DILATION
        moved = jnp.roll(extended_block, -offset, axis=2)
        inside = jnp.logical_and(columns + offset >= 0, columns + offset < column_total)
        moved = jnp.where(inside[None, None, :], moved, 0.0)
        for row_offset_tap in range(3):
            kernel_window = moved[
                :,
                row_offset_tap * KERNEL_DILATION : row_offset_tap * KERNEL_DILATION
                + slot_capacity_rows,
                :,
            ]
            running = (
                running
                + kernel_taps[3 * row_offset_tap + column_offset_tap][:, None, None] * kernel_window
            )
    return running


def section_forward(
    own_block,
    from_prev,
    received_from_next,
    row_total,
    weight_matrix,
    kernel_taps,
    shift_vector,
    gain_vector,
):
    slot_capacity_rows = own_block.shape[1]
    row_keep = (lax.iota(jnp.int32, slot_capacity_rows) < row_total).astype(jnp.float32)[
        None, :, None
    ]
    masked_block = own_block * row_keep
    extended_block = jnp.concatenate([from_prev, masked_block, jnp.zeros_like(from_prev)], axis=1)
    extended_block = lax.dynamic_update_slice(
        extended_block,
        received_from_next,
        (jnp.int32(0), row_total + KERNEL_DILATION, jnp.int32(0)),
    )
    activation = (
        depthwise(extended_block, kernel_taps, slot_capacity_rows) + shift_vector[:, None, None]
    )
    channel_mean = jnp.mean(activation, axis=0, keepdims=True)
    centered = activation - channel_mean
    variance = jnp.mean(centered * centered, axis=0, keepdims=True)
    normalized = centered * lax.rsqrt(variance + 1e-06) * gain_vector[:, None, None]
    hidden = jax.nn.gelu(normalized)
    mixing = jnp.einsum("oc,crw->orw", weight_matrix, hidden, precision=lax.Precision.HIGHEST)
    return (masked_block + mixing) * row_keep


def permute(x, pairs):
    return lax.ppermute(x, AXES, pairs)


def pack_rows(pieces, slot_rows, column_total):
    flat = jnp.concatenate([piece.reshape(-1) for piece in pieces])
    slab = slot_rows * column_total
    flat = jnp.pad(flat, (0, (-flat.shape[0]) % slab))
    return flat.reshape(-1, slot_rows, column_total)


def unpack_rows(slabs, shapes):
    flat = slabs.reshape(-1)
    out = []
    start = 0
    for shape in shapes:
        size = math.prod(shape)
        out.append(flat[start : start + size].reshape(shape))
        start += size
    return out


def seam_matrices(codes, column_total):
    columns = lax.iota(jnp.int32, column_total)
    plain = (columns[:, None] == columns[None, :]).astype(jnp.float32)
    mirror = (columns[:, None] + columns[None, :] == column_total - 1).astype(jnp.float32)
    return jnp.where((codes == 1)[:, None, None], mirror[None], plain[None])


def seam_read(rims, matrices):
    return jnp.einsum("kcrw,kwv->kcrv", rims, matrices, precision=lax.Precision.HIGHEST)


def edge_rows(own_block, row_total, matrices, pairs_of):
    slot_capacity_rows = own_block.shape[1]
    row_keep = (lax.iota(jnp.int32, slot_capacity_rows) < row_total).astype(jnp.float32)[
        None, :, None
    ]
    masked_block = own_block * row_keep
    leading_rows = masked_block[:, :KERNEL_DILATION, :]
    trailing_rows = lax.dynamic_slice_in_dim(
        masked_block, row_total - KERNEL_DILATION, KERNEL_DILATION, 1
    )
    forward_pairs, backward_pairs = pairs_of
    rims = jnp.stack([permute(trailing_rows, forward_pairs), permute(leading_rows, backward_pairs)])
    rims = seam_read(rims, matrices)
    return rims[0], rims[1]


def on_device(saved_inputs, out_grad, pointwise, kernels, shifts, gains, rows_per_tile, seam_codes):
    sections = lax.axis_size("section")
    tiles = lax.axis_size("tile")
    section_index = lax.axis_index("section")
    row_total = rows_per_tile[0]
    codes = seam_codes[0]
    lower_code = codes[0]
    upper_code = codes[1]
    micro_count = saved_inputs.shape[1]
    channels = saved_inputs.shape[2]
    slot_capacity_rows = saved_inputs.shape[3]
    column_total = saved_inputs.shape[4]
    grad_scale = 1.0 / math.sqrt(micro_count * slot_capacity_rows * tiles * column_total)
    every_section = (
        [(s * tiles + t, s * tiles + (t + 1) % tiles) for s in range(sections) for t in range(tiles)],
        [(s * tiles + (t + 1) % tiles, s * tiles + t) for s in range(sections) for t in range(tiles)],
    )
    params = (pointwise[0], kernels[0], shifts[0], gains[0])
    param_shapes = [pointwise.shape[1:], kernels.shape[1:], shifts.shape[1:], gains.shape[1:]]
    whole_top = lax.all_gather(out_grad, "section", axis=1, tiled=True)
    matrices = seam_matrices(codes, column_total)

    def apply_block(block_in, prev_in, next_in, weight_in, kernel_in, shift_in, gain_in):
        return section_forward(
            block_in, prev_in, next_in, row_total, weight_in, kernel_in, shift_in, gain_in
        )

    pulls = []
    for micro_index in range(micro_count):
        own_block = saved_inputs[0, micro_index]
        from_prev, received_from_next = edge_rows(
            own_block, row_total, matrices, every_section
        )
        _, pull = jax.vjp(apply_block, own_block, from_prev, received_from_next, *params)
        pulls.append(pull)

    def pull_at(slot_index, cotangent):
        if micro_count == 1:
            return pulls[0](cotangent)
        outs = [pull(cotangent) for pull in pulls]
        return tuple(
            sum(jnp.where(slot_index == m, o[k], 0.0) for m, o in enumerate(outs))
            for k in range(len(outs[0]))
        )

    forward_pairs, backward_pairs = every_section
    incoming = jnp.zeros((channels, slot_capacity_rows, column_total), jnp.float32)
    skip_store = jnp.zeros((micro_count, channels, slot_capacity_rows, column_total), jnp.float32)
    input_grads = jnp.zeros((micro_count, channels, slot_capacity_rows, column_total), jnp.float32)
    grad_totals = tuple(jnp.zeros(shape, jnp.float32) for shape in param_shapes)
    step_total = micro_count + sections - 1
    is_last = section_index == sections - 1
    for step_number in range(step_total):
        position = step_number - (sections - 1 - section_index)
        live_step = jnp.logical_and(position >= 0, position < micro_count)
        slot_index = jnp.clip(position, 0, micro_count - 1)
        top_grad = lax.dynamic_index_in_dim(whole_top, slot_index, 0, keepdims=False)
        grad_out = jnp.where(is_last, top_grad, incoming)
        if step_number >= sections - 1:
            carried = lax.dynamic_index_in_dim(skip_store, slot_index, 0, keepdims=False)
            grad_out = grad_out + jnp.where(section_index == 0, carried, 0.0)
        grad_own, grad_prev, grad_next, *grads = pull_at(slot_index, grad_out)
        rims = jnp.stack([grad_prev, grad_next])
        rims = seam_read(rims, matrices)
        live_sections = [
            s for s in range(sections) if 0 <= step_number - (sections - 1 - s) < micro_count
        ]
        live_forward = [(a, b) for a, b in forward_pairs if a // tiles in live_sections]
        live_backward = [(a, b) for a, b in backward_pairs if a // tiles in live_sections]
        from_next_tile = permute(rims[0], live_backward)
        from_prev_tile = permute(rims[1], live_forward)
        upper_part = lax.dynamic_update_slice_in_dim(
            jnp.zeros_like(grad_own), from_next_tile, row_total - KERNEL_DILATION, 1
        )
        lower_part = jnp.pad(
            from_prev_tile, ((0, 0), (0, slot_capacity_rows - KERNEL_DILATION), (0, 0))
        )
        input_grad = grad_own + upper_part + lower_part
        grad_totals = tuple(
            jnp.where(live_step, running + term, running) for running, term in zip(grad_totals, grads)
        )
        input_grads = jnp.where(
            live_step,
            lax.dynamic_update_index_in_dim(input_grads, input_grad, slot_index, 0),
            input_grads,
        )
        if step_number + 1 < step_total:
            incoming = permute(
                input_grad,
                [
                    (s * tiles + t, (s - 1) * tiles + t)
                    for s in live_sections
                    if s >= 1
                    for t in range(tiles)
                ],
            )
        if step_number == micro_count - 1:
            skip_store = from_behind(input_grads, "section", 1 - sections)

    partial = pack_rows(grad_totals, slot_capacity_rows, column_total) * grad_scale
    if tiles & (tiles - 1):
        partial = lax.psum(partial, "tile")
    else:
        step = 1
        while step < tiles:
            pairs = [
                (s * tiles + t, s * tiles + (t ^ step)) for s in range(sections) for t in range(tiles)
            ]
            partial = partial + permute(partial, pairs)
            step *= 2
    grad_weight, grad_kernel, grad_shift, grad_gain = unpack_rows(partial, param_shapes)
    return (
        input_grads[None],
        grad_weight[None],
        grad_kernel[None],
        grad_shift[None],
        grad_gain[None],
    )


def from_behind(block, axis, distance):
    devices = range(lax.axis_size(axis))
    route = [(i - distance, i) for i in devices if i - distance in devices]
    return lax.ppermute(block, axis, route)


def solution(mesh):
    in_specs = (
        P("section", None, None, "tile", None),
        P(None, "section", "tile", None),
        P("section", None, None),
        P("section", None, None),
        P("section", None),
        P("section", None),
        P("tile"),
        P("tile", None),
    )
    out_specs = (
        P("section", None, None, "tile", None),
        P("section", None, None),
        P("section", None, None),
        P("section", None),
        P("section", None),
    )
    return jax.shard_map(
        on_device, mesh=mesh, in_specs=in_specs, out_specs=out_specs, check_vma=False
    )
```

```python
import math

import jax
import jax.numpy as jnp
from jax import lax
from jax.sharding import PartitionSpec as P

KERNEL_DILATION = 4
AXES = ("section", "tile")


def flipped(tile_row_block, code_value):
    return jnp.where(code_value == 1, tile_row_block[..., ::-1], tile_row_block)


def depthwise(extended_block, kernel_taps, slot_capacity_rows):
    column_total = extended_block.shape[2]
    columns = lax.iota(jnp.int32, column_total)
    running = jnp.zeros((extended_block.shape[0], slot_capacity_rows, column_total), jnp.float32)
    for column_offset_tap in range(3):
        offset = (column_offset_tap - 1) * KERNEL_DILATION
        moved = jnp.roll(extended_block, -offset, axis=2)
        inside = jnp.logical_and(columns + offset >= 0, columns + offset < column_total)
        moved = jnp.where(inside[None, None, :], moved, 0.0)
        for row_offset_tap in range(3):
            kernel_window = moved[
                :,
                row_offset_tap * KERNEL_DILATION : row_offset_tap * KERNEL_DILATION
                + slot_capacity_rows,
                :,
            ]
            running = (
                running
                + kernel_taps[3 * row_offset_tap + column_offset_tap][:, None, None] * kernel_window
            )
    return running


def section_forward(
    own_block,
    from_prev,
    received_from_next,
    row_total,
    weight_matrix,
    kernel_taps,
    shift_vector,
    gain_vector,
):
    slot_capacity_rows = own_block.shape[1]
    row_keep = (lax.iota(jnp.int32, slot_capacity_rows) < row_total).astype(jnp.float32)[
        None, :, None
    ]
    masked_block = own_block * row_keep
    extended_block = jnp.concatenate([from_prev, masked_block, jnp.zeros_like(from_prev)], axis=1)
    extended_block = lax.dynamic_update_slice(
        extended_block,
        received_from_next,
        (jnp.int32(0), row_total + KERNEL_DILATION, jnp.int32(0)),
    )
    activation = (
        depthwise(extended_block, kernel_taps, slot_capacity_rows) + shift_vector[:, None, None]
    )
    channel_mean = jnp.mean(activation, axis=0, keepdims=True)
    centered = activation - channel_mean
    variance = jnp.mean(centered * centered, axis=0, keepdims=True)
    normalized = centered * lax.rsqrt(variance + 1e-06) * gain_vector[:, None, None]
    hidden = jax.nn.gelu(normalized)
    mixing = jnp.einsum("oc,crw->orw", weight_matrix, hidden, precision=lax.Precision.HIGHEST)
    return (masked_block + mixing) * row_keep


def permute(x, pairs):
    return lax.ppermute(x, AXES, pairs)


def pack_rows(pieces, slot_rows, column_total):
    flat = jnp.concatenate([piece.reshape(-1) for piece in pieces])
    slab = slot_rows * column_total
    flat = jnp.pad(flat, (0, (-flat.shape[0]) % slab))
    return flat.reshape(-1, slot_rows, column_total)


def unpack_rows(slabs, shapes):
    flat = slabs.reshape(-1)
    out = []
    start = 0
    for shape in shapes:
        size = math.prod(shape)
        out.append(flat[start : start + size].reshape(shape))
        start += size
    return out


def seam_matrices(codes, column_total):
    columns = lax.iota(jnp.int32, column_total)
    plain = (columns[:, None] == columns[None, :]).astype(jnp.float32)
    mirror = (columns[:, None] + columns[None, :] == column_total - 1).astype(jnp.float32)
    return jnp.where((codes == 1)[:, None, None], mirror[None], plain[None])


def seam_read(rims, matrices):
    return jnp.einsum("kcrw,kwv->kcrv", rims, matrices, precision=lax.Precision.HIGHEST)


def edge_rows(own_block, row_total, matrices, pairs_of):
    slot_capacity_rows = own_block.shape[1]
    row_keep = (lax.iota(jnp.int32, slot_capacity_rows) < row_total).astype(jnp.float32)[
        None, :, None
    ]
    masked_block = own_block * row_keep
    leading_rows = masked_block[:, :KERNEL_DILATION, :]
    trailing_rows = lax.dynamic_slice_in_dim(
        masked_block, row_total - KERNEL_DILATION, KERNEL_DILATION, 1
    )
    forward_pairs, backward_pairs = pairs_of
    rims = jnp.stack([permute(trailing_rows, forward_pairs), permute(leading_rows, backward_pairs)])
    rims = seam_read(rims, matrices)
    return rims[0], rims[1]


def on_device(saved_inputs, out_grad, pointwise, kernels, shifts, gains, rows_per_tile, seam_codes):
    sections = lax.axis_size("section")
    tiles = lax.axis_size("tile")
    section_index = lax.axis_index("section")
    row_total = rows_per_tile[0]
    codes = seam_codes[0]
    lower_code = codes[0]
    upper_code = codes[1]
    micro_count = saved_inputs.shape[1]
    channels = saved_inputs.shape[2]
    slot_capacity_rows = saved_inputs.shape[3]
    column_total = saved_inputs.shape[4]
    grad_scale = 1.0 / math.sqrt(micro_count * slot_capacity_rows * tiles * column_total)
    every_section = (
        [(s * tiles + t, s * tiles + (t + 1) % tiles) for s in range(sections) for t in range(tiles)],
        [(s * tiles + (t + 1) % tiles, s * tiles + t) for s in range(sections) for t in range(tiles)],
    )
    params = (pointwise[0], kernels[0], shifts[0], gains[0])
    param_shapes = [pointwise.shape[1:], kernels.shape[1:], shifts.shape[1:], gains.shape[1:]]
    last = sections - 1
    whole_top = jnp.concatenate(
        [
            out_grad
            if b == last
            else permute(out_grad, [(b * tiles + t, last * tiles + t) for t in range(tiles)])
            for b in range(sections)
        ],
        axis=1,
    )
    matrices = seam_matrices(codes, column_total)

    def apply_block(block_in, prev_in, next_in, weight_in, kernel_in, shift_in, gain_in):
        return section_forward(
            block_in, prev_in, next_in, row_total, weight_in, kernel_in, shift_in, gain_in
        )

    pulls = []
    for micro_index in range(micro_count):
        own_block = saved_inputs[0, micro_index]
        from_prev, received_from_next = edge_rows(
            own_block, row_total, matrices, every_section
        )
        _, pull = jax.vjp(apply_block, own_block, from_prev, received_from_next, *params)
        pulls.append(pull)

    def pull_at(slot_index, cotangent):
        if micro_count == 1:
            return pulls[0](cotangent)
        outs = [pull(cotangent) for pull in pulls]
        return tuple(
            sum(jnp.where(slot_index == m, o[k], 0.0) for m, o in enumerate(outs))
            for k in range(len(outs[0]))
        )

    forward_pairs, backward_pairs = every_section
    incoming = jnp.zeros((channels, slot_capacity_rows, column_total), jnp.float32)
    skip_store = jnp.zeros((micro_count, channels, slot_capacity_rows, column_total), jnp.float32)
    input_grads = jnp.zeros((micro_count, channels, slot_capacity_rows, column_total), jnp.float32)
    grad_totals = tuple(jnp.zeros(shape, jnp.float32) for shape in param_shapes)
    step_total = micro_count + sections - 1
    is_last = section_index == sections - 1
    for step_number in range(step_total):
        position = step_number - (sections - 1 - section_index)
        live_step = jnp.logical_and(position >= 0, position < micro_count)
        slot_index = jnp.clip(position, 0, micro_count - 1)
        top_grad = lax.dynamic_index_in_dim(whole_top, slot_index, 0, keepdims=False)
        grad_out = jnp.where(is_last, top_grad, incoming)
        if step_number >= sections - 1:
            carried = lax.dynamic_index_in_dim(skip_store, slot_index, 0, keepdims=False)
            grad_out = grad_out + jnp.where(section_index == 0, carried, 0.0)
        grad_own, grad_prev, grad_next, *grads = pull_at(slot_index, grad_out)
        rims = jnp.stack([grad_prev, grad_next])
        rims = seam_read(rims, matrices)
        live_sections = [
            s for s in range(sections) if 0 <= step_number - (sections - 1 - s) < micro_count
        ]
        live_forward = [(a, b) for a, b in forward_pairs if a // tiles in live_sections]
        live_backward = [(a, b) for a, b in backward_pairs if a // tiles in live_sections]
        from_next_tile = permute(rims[0], live_backward)
        from_prev_tile = permute(rims[1], live_forward)
        upper_part = lax.dynamic_update_slice_in_dim(
            jnp.zeros_like(grad_own), from_next_tile, row_total - KERNEL_DILATION, 1
        )
        lower_part = jnp.pad(
            from_prev_tile, ((0, 0), (0, slot_capacity_rows - KERNEL_DILATION), (0, 0))
        )
        input_grad = grad_own + upper_part + lower_part
        grad_totals = tuple(
            jnp.where(live_step, running + term, running) for running, term in zip(grad_totals, grads)
        )
        input_grads = jnp.where(
            live_step,
            lax.dynamic_update_index_in_dim(input_grads, input_grad, slot_index, 0),
            input_grads,
        )
        if step_number + 1 < step_total:
            hop = [
                (s * tiles + t, (s - 1) * tiles + t)
                for s in live_sections
                if s >= 1
                for t in range(tiles)
            ]
            if all(s % 2 == 0 for s in live_sections):
                half = channels // 2
                incoming = jnp.concatenate(
                    [permute(input_grad[:half], hop), permute(input_grad[half:], hop)], axis=0
                )
            else:
                incoming = permute(input_grad, hop)
        if step_number == micro_count - 1:
            skip_store = from_behind(input_grads, "section", 1 - sections)

    partial = pack_rows(grad_totals, slot_capacity_rows, column_total) * grad_scale
    if tiles & (tiles - 1):
        partial = lax.psum(partial, "tile")
    else:
        step = 1
        while step < tiles:
            pairs = [
                (s * tiles + t, s * tiles + (t ^ step)) for s in range(sections) for t in range(tiles)
            ]
            partial = partial + permute(partial, pairs)
            step *= 2
    grad_weight, grad_kernel, grad_shift, grad_gain = unpack_rows(partial, param_shapes)
    return (
        input_grads[None],
        grad_weight[None],
        grad_kernel[None],
        grad_shift[None],
        grad_gain[None],
    )


def from_behind(block, axis, distance):
    devices = range(lax.axis_size(axis))
    route = [(i - distance, i) for i in devices if i - distance in devices]
    return lax.ppermute(block, axis, route)


def solution(mesh):
    in_specs = (
        P("section", None, None, "tile", None),
        P(None, "section", "tile", None),
        P("section", None, None),
        P("section", None, None),
        P("section", None),
        P("section", None),
        P("tile"),
        P("tile", None),
    )
    out_specs = (
        P("section", None, None, "tile", None),
        P("section", None, None),
        P("section", None, None),
        P("section", None),
        P("section", None),
    )
    return jax.shard_map(
        on_device, mesh=mesh, in_specs=in_specs, out_specs=out_specs, check_vma=False
    )
```

```python
import math

import jax
import jax.numpy as jnp
from jax import lax
from jax.sharding import PartitionSpec as P


KERNEL_DILATION = 4
AXES = ("section", "tile")


def depthwise(extended_block, kernel_taps, slot_capacity_rows):
    column_total = extended_block.shape[2]
    columns = lax.iota(jnp.int32, column_total)
    running = jnp.zeros((extended_block.shape[0], slot_capacity_rows, column_total), jnp.float32)
    for column_offset_tap in range(3):
        offset = (column_offset_tap - 1) * KERNEL_DILATION
        moved = jnp.roll(extended_block, -offset, axis=2)
        inside = jnp.logical_and(columns + offset >= 0, columns + offset < column_total)
        moved = jnp.where(inside[None, None, :], moved, 0.0)
        for row_offset_tap in range(3):
            kernel_window = moved[
                :,
                row_offset_tap * KERNEL_DILATION : row_offset_tap * KERNEL_DILATION
                + slot_capacity_rows,
                :,
            ]
            running = (
                running
                + kernel_taps[3 * row_offset_tap + column_offset_tap][:, None, None] * kernel_window
            )
    return running


def section_forward(
    own_block,
    from_prev,
    received_from_next,
    row_total,
    weight_matrix,
    kernel_taps,
    shift_vector,
    gain_vector,
):
    slot_capacity_rows = own_block.shape[1]
    row_keep = (lax.iota(jnp.int32, slot_capacity_rows) < row_total).astype(jnp.float32)[
        None, :, None
    ]
    masked_block = own_block * row_keep
    extended_block = jnp.concatenate([from_prev, masked_block, jnp.zeros_like(from_prev)], axis=1)
    extended_block = lax.dynamic_update_slice(
        extended_block,
        received_from_next,
        (jnp.int32(0), row_total + KERNEL_DILATION, jnp.int32(0)),
    )
    activation = (
        depthwise(extended_block, kernel_taps, slot_capacity_rows) + shift_vector[:, None, None]
    )
    channel_mean = jnp.mean(activation, axis=0, keepdims=True)
    centered = activation - channel_mean
    variance = jnp.mean(centered * centered, axis=0, keepdims=True)
    normalized = centered * lax.rsqrt(variance + 1e-06) * gain_vector[:, None, None]
    hidden = jax.nn.gelu(normalized)
    mixing = jnp.einsum("oc,crw->orw", weight_matrix, hidden, precision=lax.Precision.HIGHEST)
    return (masked_block + mixing) * row_keep


def permute(x, pairs):
    return lax.ppermute(x, AXES, pairs)


def pack_rows(pieces, slot_rows, column_total):
    flat = jnp.concatenate([piece.reshape(-1) for piece in pieces])
    slab = slot_rows * column_total
    flat = jnp.pad(flat, (0, (-flat.shape[0]) % slab))
    return flat.reshape(-1, slot_rows, column_total)


def unpack_rows(slabs, shapes):
    flat = slabs.reshape(-1)
    out = []
    start = 0
    for shape in shapes:
        size = math.prod(shape)
        out.append(flat[start : start + size].reshape(shape))
        start += size
    return out


def seam_matrices(codes, column_total):
    columns = lax.iota(jnp.int32, column_total)
    plain = (columns[:, None] == columns[None, :]).astype(jnp.float32)
    mirror = (columns[:, None] + columns[None, :] == column_total - 1).astype(jnp.float32)
    return jnp.where((codes == 1)[:, None, None], mirror[None], plain[None])


def seam_read(rims, matrices):
    return jnp.einsum("kcrw,kwv->kcrv", rims, matrices, precision=lax.Precision.HIGHEST)


def edge_rows(own_block, row_total, matrices, pairs_of):
    slot_capacity_rows = own_block.shape[1]
    row_keep = (lax.iota(jnp.int32, slot_capacity_rows) < row_total).astype(jnp.float32)[
        None, :, None
    ]
    masked_block = own_block * row_keep
    leading_rows = masked_block[:, :KERNEL_DILATION, :]
    trailing_rows = lax.dynamic_slice_in_dim(
        masked_block, row_total - KERNEL_DILATION, KERNEL_DILATION, 1
    )
    forward_pairs, backward_pairs = pairs_of
    rims = jnp.stack([permute(trailing_rows, forward_pairs), permute(leading_rows, backward_pairs)])
    rims = seam_read(rims, matrices)
    return rims[0], rims[1]


def cell_mix(activation, weight_matrix, gain_vector):
    channel_mean = jnp.mean(activation, axis=0, keepdims=True)
    centered = activation - channel_mean
    variance = jnp.mean(centered * centered, axis=0, keepdims=True)
    normalized = centered * lax.rsqrt(variance + 1e-06) * gain_vector[:, None, None]
    hidden = jax.nn.gelu(normalized)
    return jnp.einsum("oc,crw->orw", weight_matrix, hidden, precision=lax.Precision.HIGHEST)


def activation_of(own_block, from_prev, received_from_next, row_total, kernel_taps, shift_vector):
    slot_capacity_rows = own_block.shape[1]
    row_keep = (lax.iota(jnp.int32, slot_capacity_rows) < row_total).astype(jnp.float32)[
        None, :, None
    ]
    masked_block = own_block * row_keep
    extended_block = jnp.concatenate([from_prev, masked_block, jnp.zeros_like(from_prev)], axis=1)
    extended_block = lax.dynamic_update_slice(
        extended_block,
        received_from_next,
        (jnp.int32(0), row_total + KERNEL_DILATION, jnp.int32(0)),
    )
    return depthwise(extended_block, kernel_taps, slot_capacity_rows) + shift_vector[:, None, None]


def edge_slabs(field, row_total):
    return jnp.concatenate(
        [
            field[:, :KERNEL_DILATION, :],
            lax.dynamic_slice_in_dim(field, row_total - KERNEL_DILATION, KERNEL_DILATION, 1),
        ],
        axis=1,
    )


def rim_grads(edge_grad, kernel_taps):
    column_total = edge_grad.shape[2]
    columns = lax.iota(jnp.int32, column_total)
    lower = edge_grad[:, :KERNEL_DILATION, :]
    upper = edge_grad[:, KERNEL_DILATION:, :]
    grad_prev = jnp.zeros_like(lower)
    grad_next = jnp.zeros_like(upper)
    for column_offset_tap in range(3):
        offset = (column_offset_tap - 1) * KERNEL_DILATION
        inside = jnp.logical_and(columns - offset >= 0, columns - offset < column_total)
        moved_lower = jnp.where(inside[None, None, :], jnp.roll(lower, offset, axis=2), 0.0)
        moved_upper = jnp.where(inside[None, None, :], jnp.roll(upper, offset, axis=2), 0.0)
        grad_prev = grad_prev + kernel_taps[column_offset_tap][:, None, None] * moved_lower
        grad_next = grad_next + kernel_taps[6 + column_offset_tap][:, None, None] * moved_upper
    return grad_prev, grad_next


def on_device(saved_inputs, out_grad, pointwise, kernels, shifts, gains, rows_per_tile, seam_codes):
    sections = lax.axis_size("section")
    tiles = lax.axis_size("tile")
    section_index = lax.axis_index("section")
    row_total = rows_per_tile[0]
    codes = seam_codes[0]
    micro_count = saved_inputs.shape[1]
    channels = saved_inputs.shape[2]
    slot_capacity_rows = saved_inputs.shape[3]
    column_total = saved_inputs.shape[4]
    grad_scale = 1.0 / math.sqrt(micro_count * slot_capacity_rows * tiles * column_total)
    every_section = (
        [(s * tiles + t, s * tiles + (t + 1) % tiles) for s in range(sections) for t in range(tiles)],
        [(s * tiles + (t + 1) % tiles, s * tiles + t) for s in range(sections) for t in range(tiles)],
    )
    params = (pointwise[0], kernels[0], shifts[0], gains[0])
    param_shapes = [pointwise.shape[1:], kernels.shape[1:], shifts.shape[1:], gains.shape[1:]]
    whole_top = lax.all_gather(out_grad, "section", axis=1, tiled=True)
    matrices = seam_matrices(codes, column_total)

    def apply_block(block_in, prev_in, next_in, weight_in, kernel_in, shift_in, gain_in):
        return section_forward(
            block_in, prev_in, next_in, row_total, weight_in, kernel_in, shift_in, gain_in
        )

    pulls = []
    edge_pulls = []
    for micro_index in range(micro_count):
        own_block = saved_inputs[0, micro_index]
        from_prev, received_from_next = edge_rows(
            own_block, row_total, matrices, every_section
        )
        _, pull = jax.vjp(apply_block, own_block, from_prev, received_from_next, *params)
        pulls.append(pull)
        activation = activation_of(
            own_block, from_prev, received_from_next, row_total, params[1], params[2]
        )
        _, edge_pull = jax.vjp(
            lambda edge: cell_mix(edge, params[0], params[3]), edge_slabs(activation, row_total)
        )
        edge_pulls.append(edge_pull)

    def pull_at(slot_index, cotangent):
        if micro_count == 1:
            return pulls[0](cotangent)
        outs = [pull(cotangent) for pull in pulls]
        return tuple(
            sum(jnp.where(slot_index == m, o[k], 0.0) for m, o in enumerate(outs))
            for k in range(len(outs[0]))
        )

    forward_pairs, backward_pairs = every_section
    incoming = jnp.zeros((channels, slot_capacity_rows, column_total), jnp.float32)
    skip_store = jnp.zeros((micro_count, channels, slot_capacity_rows, column_total), jnp.float32)
    input_grads = jnp.zeros((micro_count, channels, slot_capacity_rows, column_total), jnp.float32)
    grad_totals = tuple(jnp.zeros(shape, jnp.float32) for shape in param_shapes)
    step_total = micro_count + sections - 1
    is_last = section_index == sections - 1
    for step_number in range(step_total):
      position = step_number - (sections - 1 - section_index)
      live_step = jnp.logical_and(position >= 0, position < micro_count)
      slot_index = jnp.clip(position, 0, micro_count - 1)
      top_grad = lax.dynamic_index_in_dim(whole_top, slot_index, 0, keepdims=False)
      grad_out = jnp.where(is_last, top_grad, incoming)
      if step_number >= sections - 1:
          carried = lax.dynamic_index_in_dim(skip_store, slot_index, 0, keepdims=False)
          grad_out = grad_out + jnp.where(section_index == 0, carried, 0.0)
      edge_grads = [edge_pull(edge_slabs(grad_out, row_total))[0] for edge_pull in edge_pulls]
      edge_grad = edge_grads[0]
      for m in range(1, micro_count):
          edge_grad = jnp.where(slot_index == m, edge_grads[m], edge_grad)
      rims = seam_read(jnp.stack(rim_grads(edge_grad, params[1])), matrices)
      grad_out, rims = lax.optimization_barrier((grad_out, rims))
      grad_own, _, _, *grads = pull_at(slot_index, grad_out)
      live_sections = [
          s for s in range(sections) if 0 <= step_number - (sections - 1 - s) < micro_count
      ]
      live_forward = [(a, b) for a, b in forward_pairs if a // tiles in live_sections]
      live_backward = [(a, b) for a, b in backward_pairs if a // tiles in live_sections]
      from_next_tile = permute(rims[0], live_backward)
      from_prev_tile = permute(rims[1], live_forward)
      upper_part = lax.dynamic_update_slice_in_dim(
          jnp.zeros_like(grad_own), from_next_tile, row_total - KERNEL_DILATION, 1
      )
      lower_part = jnp.pad(
          from_prev_tile, ((0, 0), (0, slot_capacity_rows - KERNEL_DILATION), (0, 0))
      )
      input_grad = grad_own + upper_part + lower_part
      grad_totals = tuple(
          jnp.where(live_step, running + term, running) for running, term in zip(grad_totals, grads)
      )
      input_grads = jnp.where(
          live_step,
          lax.dynamic_update_index_in_dim(input_grads, input_grad, slot_index, 0),
          input_grads,
      )
      if step_number + 1 < step_total:
          incoming = permute(
              input_grad,
              [
                  (s * tiles + t, (s - 1) * tiles + t)
                  for s in live_sections
                  if s >= 1
                  for t in range(tiles)
              ],
          )
      if step_number == micro_count - 1:
          skip_store = from_behind(input_grads, "section", 1 - sections)

    partial = pack_rows(grad_totals, slot_capacity_rows, column_total) * grad_scale
    if tiles & (tiles - 1):
        partial = lax.psum(partial, "tile")
    else:
        step = 1
        while step < tiles:
            pairs = [
                (s * tiles + t, s * tiles + (t ^ step)) for s in range(sections) for t in range(tiles)
            ]
            partial = partial + permute(partial, pairs)
            step *= 2
    grad_weight, grad_kernel, grad_shift, grad_gain = unpack_rows(partial, param_shapes)
    return (
        input_grads[None],
        grad_weight[None],
        grad_kernel[None],
        grad_shift[None],
        grad_gain[None],
    )


def from_behind(block, axis, distance):
    devices = range(lax.axis_size(axis))
    route = [(i - distance, i) for i in devices if i - distance in devices]
    return lax.ppermute(block, axis, route)


def solution(mesh):
    in_specs = (
        P("section", None, None, "tile", None),
        P(None, "section", "tile", None),
        P("section", None, None),
        P("section", None, None),
        P("section", None),
        P("section", None),
        P("tile"),
        P("tile", None),
    )
    out_specs = (
        P("section", None, None, "tile", None),
        P("section", None, None),
        P("section", None, None),
        P("section", None),
        P("section", None),
    )
    return jax.shard_map(
        on_device, mesh=mesh, in_specs=in_specs, out_specs=out_specs, check_vma=False
    )
```

```python
import math

import jax
import jax.numpy as jnp
from jax import lax
from jax.sharding import PartitionSpec as P


KERNEL_DILATION = 4
AXES = ("section", "tile")


def depthwise(extended_block, kernel_taps, slot_capacity_rows):
    column_total = extended_block.shape[2]
    columns = lax.iota(jnp.int32, column_total)
    running = jnp.zeros((extended_block.shape[0], slot_capacity_rows, column_total), jnp.float32)
    for column_offset_tap in range(3):
        offset = (column_offset_tap - 1) * KERNEL_DILATION
        moved = jnp.roll(extended_block, -offset, axis=2)
        inside = jnp.logical_and(columns + offset >= 0, columns + offset < column_total)
        moved = jnp.where(inside[None, None, :], moved, 0.0)
        for row_offset_tap in range(3):
            kernel_window = moved[
                :,
                row_offset_tap * KERNEL_DILATION : row_offset_tap * KERNEL_DILATION
                + slot_capacity_rows,
                :,
            ]
            running = (
                running
                + kernel_taps[3 * row_offset_tap + column_offset_tap][:, None, None] * kernel_window
            )
    return running


def section_forward(
    own_block,
    from_prev,
    received_from_next,
    row_total,
    weight_matrix,
    kernel_taps,
    shift_vector,
    gain_vector,
):
    slot_capacity_rows = own_block.shape[1]
    row_keep = (lax.iota(jnp.int32, slot_capacity_rows) < row_total).astype(jnp.float32)[
        None, :, None
    ]
    masked_block = own_block * row_keep
    extended_block = jnp.concatenate([from_prev, masked_block, jnp.zeros_like(from_prev)], axis=1)
    extended_block = lax.dynamic_update_slice(
        extended_block,
        received_from_next,
        (jnp.int32(0), row_total + KERNEL_DILATION, jnp.int32(0)),
    )
    activation = (
        depthwise(extended_block, kernel_taps, slot_capacity_rows) + shift_vector[:, None, None]
    )
    channel_mean = jnp.mean(activation, axis=0, keepdims=True)
    centered = activation - channel_mean
    variance = jnp.mean(centered * centered, axis=0, keepdims=True)
    normalized = centered * lax.rsqrt(variance + 1e-06) * gain_vector[:, None, None]
    hidden = jax.nn.gelu(normalized)
    mixing = jnp.einsum("oc,crw->orw", weight_matrix, hidden, precision=lax.Precision.HIGHEST)
    return (masked_block + mixing) * row_keep


def permute(x, pairs):
    return lax.ppermute(x, AXES, pairs)


def pack_rows(pieces, slot_rows, column_total):
    flat = jnp.concatenate([piece.reshape(-1) for piece in pieces])
    slab = slot_rows * column_total
    flat = jnp.pad(flat, (0, (-flat.shape[0]) % slab))
    return flat.reshape(-1, slot_rows, column_total)


def unpack_rows(slabs, shapes):
    flat = slabs.reshape(-1)
    out = []
    start = 0
    for shape in shapes:
        size = math.prod(shape)
        out.append(flat[start : start + size].reshape(shape))
        start += size
    return out


def seam_matrices(codes, column_total):
    columns = lax.iota(jnp.int32, column_total)
    plain = (columns[:, None] == columns[None, :]).astype(jnp.float32)
    mirror = (columns[:, None] + columns[None, :] == column_total - 1).astype(jnp.float32)
    return jnp.where((codes == 1)[:, None, None], mirror[None], plain[None])


def seam_read(rims, matrices):
    return jnp.einsum("kcrw,kwv->kcrv", rims, matrices, precision=lax.Precision.HIGHEST)


def edge_rows(own_block, row_total, matrices, pairs_of):
    slot_capacity_rows = own_block.shape[1]
    row_keep = (lax.iota(jnp.int32, slot_capacity_rows) < row_total).astype(jnp.float32)[
        None, :, None
    ]
    masked_block = own_block * row_keep
    leading_rows = masked_block[:, :KERNEL_DILATION, :]
    trailing_rows = lax.dynamic_slice_in_dim(
        masked_block, row_total - KERNEL_DILATION, KERNEL_DILATION, 1
    )
    forward_pairs, backward_pairs = pairs_of
    rims = jnp.stack([permute(trailing_rows, forward_pairs), permute(leading_rows, backward_pairs)])
    rims = seam_read(rims, matrices)
    return rims[0], rims[1]


def on_device(saved_inputs, out_grad, pointwise, kernels, shifts, gains, rows_per_tile, seam_codes):
    sections = lax.axis_size("section")
    tiles = lax.axis_size("tile")
    section_index = lax.axis_index("section")
    row_total = rows_per_tile[0]
    codes = seam_codes[0]
    micro_count = saved_inputs.shape[1]
    channels = saved_inputs.shape[2]
    slot_capacity_rows = saved_inputs.shape[3]
    column_total = saved_inputs.shape[4]
    grad_scale = 1.0 / math.sqrt(micro_count * slot_capacity_rows * tiles * column_total)
    every_section = (
        [(s * tiles + t, s * tiles + (t + 1) % tiles) for s in range(sections) for t in range(tiles)],
        [(s * tiles + (t + 1) % tiles, s * tiles + t) for s in range(sections) for t in range(tiles)],
    )
    params = (pointwise[0], kernels[0], shifts[0], gains[0])
    param_shapes = [pointwise.shape[1:], kernels.shape[1:], shifts.shape[1:], gains.shape[1:]]
    whole_top = lax.all_gather(out_grad, "section", axis=1, tiled=True)
    matrices = seam_matrices(codes, column_total)

    def apply_block(block_in, prev_in, next_in, weight_in, kernel_in, shift_in, gain_in):
        return section_forward(
            block_in, prev_in, next_in, row_total, weight_in, kernel_in, shift_in, gain_in
        )

    pulls = []
    for micro_index in range(micro_count):
        own_block = saved_inputs[0, micro_index]
        from_prev, received_from_next = edge_rows(
            own_block, row_total, matrices, every_section
        )
        _, pull = jax.vjp(apply_block, own_block, from_prev, received_from_next, *params)
        pulls.append(pull)

    def pull_at(slot_index, cotangent):
        if micro_count == 1:
            return pulls[0](cotangent)
        outs = [pull(cotangent) for pull in pulls]
        return tuple(
            sum(jnp.where(slot_index == m, o[k], 0.0) for m, o in enumerate(outs))
            for k in range(len(outs[0]))
        )

    forward_pairs, backward_pairs = every_section
    incoming = jnp.zeros((channels, slot_capacity_rows, column_total), jnp.float32)
    skip_store = jnp.zeros((micro_count, channels, slot_capacity_rows, column_total), jnp.float32)
    input_grads = jnp.zeros((micro_count, channels, slot_capacity_rows, column_total), jnp.float32)
    grad_totals = tuple(jnp.zeros(shape, jnp.float32) for shape in param_shapes)
    step_total = micro_count + sections - 1
    is_last = section_index == sections - 1
    for step_number in range(step_total):
        position = step_number - (sections - 1 - section_index)
        live_step = jnp.logical_and(position >= 0, position < micro_count)
        slot_index = jnp.clip(position, 0, micro_count - 1)
        top_grad = lax.dynamic_index_in_dim(whole_top, slot_index, 0, keepdims=False)
        grad_out = jnp.where(is_last, top_grad, incoming)
        if step_number >= sections - 1:
            carried = lax.dynamic_index_in_dim(skip_store, slot_index, 0, keepdims=False)
            grad_out = grad_out + jnp.where(section_index == 0, carried, 0.0)
        grad_own, grad_prev, grad_next, *grads = pull_at(slot_index, grad_out)
        rims = jnp.stack([grad_prev, grad_next])
        rims = seam_read(rims, matrices)
        live_sections = [
            s for s in range(sections) if 0 <= step_number - (sections - 1 - s) < micro_count
        ]
        live_forward = [(a, b) for a, b in forward_pairs if a // tiles in live_sections]
        live_backward = [(a, b) for a, b in backward_pairs if a // tiles in live_sections]
        from_next_tile = permute(rims[0], live_backward)
        from_prev_tile = permute(rims[1], live_forward)
        upper_part = lax.dynamic_update_slice_in_dim(
            jnp.zeros_like(grad_own), from_next_tile, row_total - KERNEL_DILATION, 1
        )
        lower_part = jnp.pad(
            from_prev_tile, ((0, 0), (0, slot_capacity_rows - KERNEL_DILATION), (0, 0))
        )
        input_grad = grad_own + upper_part + lower_part
        grad_totals = tuple(
            jnp.where(live_step, running + term, running) for running, term in zip(grad_totals, grads)
        )
        input_grads = jnp.where(
            live_step,
            lax.dynamic_update_index_in_dim(input_grads, input_grad, slot_index, 0),
            input_grads,
        )
        if step_number + 1 < step_total:
            incoming = permute(
                input_grad,
                [
                    (s * tiles + t, (s - 1) * tiles + t)
                    for s in live_sections
                    if s >= 1
                    for t in range(tiles)
                ],
            )
        if step_number == micro_count - 1:
            skip_store = from_behind(input_grads, "section", 1 - sections)

    partial = pack_rows(grad_totals, slot_capacity_rows, column_total) * grad_scale
    if tiles & (tiles - 1):
        partial = lax.psum(partial, "tile")
    else:
        step = 1
        while step < tiles:
            pairs = [
                (s * tiles + t, s * tiles + (t ^ step))
                for s in range(sections)
                for t in range(tiles)
            ]
            partial = partial + permute(partial, pairs)
            step *= 2
    grad_weight, grad_kernel, grad_shift, grad_gain = unpack_rows(partial, param_shapes)
    return (
        input_grads[None],
        grad_weight[None],
        grad_kernel[None],
        grad_shift[None],
        grad_gain[None],
    )


def from_behind(block, axis, distance):
    devices = range(lax.axis_size(axis))
    route = [(i - distance, i) for i in devices if i - distance in devices]
    return lax.ppermute(block, axis, route)


def solution(mesh):
    in_specs = (
        P("section", None, None, "tile", None),
        P(None, "section", "tile", None),
        P("section", None, None),
        P("section", None, None),
        P("section", None),
        P("section", None),
        P("tile"),
        P("tile", None),
    )
    out_specs = (
        P("section", None, None, "tile", None),
        P("section", None, None),
        P("section", None, None),
        P("section", None),
        P("section", None),
    )
    return jax.shard_map(
        on_device, mesh=mesh, in_specs=in_specs, out_specs=out_specs, check_vma=False
    )
```

```python
import math

import jax
import jax.numpy as jnp
from jax import lax
from jax.sharding import PartitionSpec as P


KERNEL_DILATION = 4
AXES = ("section", "tile")


def depthwise(extended_block, kernel_taps, slot_capacity_rows):
    column_total = extended_block.shape[2]
    columns = lax.iota(jnp.int32, column_total)
    running = jnp.zeros((extended_block.shape[0], slot_capacity_rows, column_total), jnp.float32)
    for column_offset_tap in range(3):
        offset = (column_offset_tap - 1) * KERNEL_DILATION
        moved = jnp.roll(extended_block, -offset, axis=2)
        inside = jnp.logical_and(columns + offset >= 0, columns + offset < column_total)
        moved = jnp.where(inside[None, None, :], moved, 0.0)
        for row_offset_tap in range(3):
            kernel_window = moved[
                :,
                row_offset_tap * KERNEL_DILATION : row_offset_tap * KERNEL_DILATION
                + slot_capacity_rows,
                :,
            ]
            running = (
                running
                + kernel_taps[3 * row_offset_tap + column_offset_tap][:, None, None] * kernel_window
            )
    return running


def section_forward(
    own_block,
    from_prev,
    received_from_next,
    row_total,
    weight_matrix,
    kernel_taps,
    shift_vector,
    gain_vector,
):
    slot_capacity_rows = own_block.shape[1]
    row_keep = (lax.iota(jnp.int32, slot_capacity_rows) < row_total).astype(jnp.float32)[
        None, :, None
    ]
    masked_block = own_block * row_keep
    extended_block = jnp.concatenate([from_prev, masked_block, jnp.zeros_like(from_prev)], axis=1)
    extended_block = lax.dynamic_update_slice(
        extended_block,
        received_from_next,
        (jnp.int32(0), row_total + KERNEL_DILATION, jnp.int32(0)),
    )
    activation = (
        depthwise(extended_block, kernel_taps, slot_capacity_rows) + shift_vector[:, None, None]
    )
    channel_mean = jnp.mean(activation, axis=0, keepdims=True)
    centered = activation - channel_mean
    variance = jnp.mean(centered * centered, axis=0, keepdims=True)
    normalized = centered * lax.rsqrt(variance + 1e-06) * gain_vector[:, None, None]
    hidden = jax.nn.gelu(normalized)
    mixing = jnp.einsum("oc,crw->orw", weight_matrix, hidden, precision=lax.Precision.HIGHEST)
    return (masked_block + mixing) * row_keep


def permute(x, pairs):
    return lax.ppermute(x, AXES, pairs)


def pack_rows(pieces, slot_rows, column_total):
    flat = jnp.concatenate([piece.reshape(-1) for piece in pieces])
    slab = slot_rows * column_total
    flat = jnp.pad(flat, (0, (-flat.shape[0]) % slab))
    return flat.reshape(-1, slot_rows, column_total)


def unpack_rows(slabs, shapes):
    flat = slabs.reshape(-1)
    out = []
    start = 0
    for shape in shapes:
        size = math.prod(shape)
        out.append(flat[start : start + size].reshape(shape))
        start += size
    return out


def seam_matrices(codes, column_total):
    columns = lax.iota(jnp.int32, column_total)
    plain = (columns[:, None] == columns[None, :]).astype(jnp.float32)
    mirror = (columns[:, None] + columns[None, :] == column_total - 1).astype(jnp.float32)
    return jnp.where((codes == 1)[:, None, None], mirror[None], plain[None])


def seam_read(rims, matrices):
    return jnp.einsum("kcrw,kwv->kcrv", rims, matrices, precision=lax.Precision.HIGHEST)


def edge_rows(own_block, row_total, matrices, pairs_of):
    slot_capacity_rows = own_block.shape[1]
    row_keep = (lax.iota(jnp.int32, slot_capacity_rows) < row_total).astype(jnp.float32)[
        None, :, None
    ]
    masked_block = own_block * row_keep
    leading_rows = masked_block[:, :KERNEL_DILATION, :]
    trailing_rows = lax.dynamic_slice_in_dim(
        masked_block, row_total - KERNEL_DILATION, KERNEL_DILATION, 1
    )
    forward_pairs, backward_pairs = pairs_of
    rims = jnp.stack([permute(trailing_rows, forward_pairs), permute(leading_rows, backward_pairs)])
    rims = seam_read(rims, matrices)
    return rims[0], rims[1]


def on_device(saved_inputs, out_grad, pointwise, kernels, shifts, gains, rows_per_tile, seam_codes):
    sections = lax.axis_size("section")
    tiles = lax.axis_size("tile")
    section_index = lax.axis_index("section")
    row_total = rows_per_tile[0]
    codes = seam_codes[0]
    micro_count = saved_inputs.shape[1]
    channels = saved_inputs.shape[2]
    slot_capacity_rows = saved_inputs.shape[3]
    column_total = saved_inputs.shape[4]
    grad_scale = 1.0 / math.sqrt(micro_count * slot_capacity_rows * tiles * column_total)
    every_section = (
        [(s * tiles + t, s * tiles + (t + 1) % tiles) for s in range(sections) for t in range(tiles)],
        [(s * tiles + (t + 1) % tiles, s * tiles + t) for s in range(sections) for t in range(tiles)],
    )
    params = (pointwise[0], kernels[0], shifts[0], gains[0])
    param_shapes = [pointwise.shape[1:], kernels.shape[1:], shifts.shape[1:], gains.shape[1:]]
    whole_top = lax.all_gather(out_grad, "section", axis=1, tiled=True)
    matrices = seam_matrices(codes, column_total)

    def apply_block(block_in, prev_in, next_in, weight_in, kernel_in, shift_in, gain_in):
        return section_forward(
            block_in, prev_in, next_in, row_total, weight_in, kernel_in, shift_in, gain_in
        )

    pulls = []
    for micro_index in range(micro_count):
        own_block = saved_inputs[0, micro_index]
        from_prev, received_from_next = edge_rows(
            own_block, row_total, matrices, every_section
        )
        _, pull = jax.vjp(apply_block, own_block, from_prev, received_from_next, *params)
        pulls.append(pull)

    forward_pairs, backward_pairs = every_section

    def assemble(grad_own, from_next_tile, from_prev_tile):
        upper_part = lax.dynamic_update_slice_in_dim(
            jnp.zeros_like(grad_own), from_next_tile, row_total - KERNEL_DILATION, 1
        )
        lower_part = jnp.pad(
            from_prev_tile, ((0, 0), (0, slot_capacity_rows - KERNEL_DILATION), (0, 0))
        )
        return grad_own + upper_part + lower_part

    def send_with_rims(grad_own, rims, source, target):
        own = permute(grad_own, [(source * tiles + t, target * tiles + t) for t in range(tiles)])
        upper = permute(
            rims[0],
            [(source * tiles + (t + 1) % tiles, target * tiles + t) for t in range(tiles)],
        )
        lower = permute(
            rims[1],
            [(source * tiles + t, target * tiles + (t + 1) % tiles) for t in range(tiles)],
        )
        return assemble(own, upper, lower)

    def halo_within(rims, members):
        backward = [(a, b) for a, b in backward_pairs if a // tiles in members]
        forward = [(a, b) for a, b in forward_pairs if a // tiles in members]
        return permute(rims[0], backward), permute(rims[1], forward)

    assert micro_count == 1
    zero_block = jnp.zeros((channels, slot_capacity_rows, column_total), jnp.float32)
    incoming = zero_block
    skip_grad = zero_block
    own_hold = zero_block
    rims_hold = jnp.zeros((2, channels, KERNEL_DILATION, column_total), jnp.float32)
    grad_totals = tuple(jnp.zeros(shape, jnp.float32) for shape in param_shapes)
    is_last = section_index == sections - 1
    for step_number in range(sections):
        live = sections - 1 - step_number
        live_step = section_index == live
        grad_out = jnp.where(is_last, whole_top[0], incoming)
        if live == 0:
            grad_out = grad_out + jnp.where(section_index == 0, skip_grad, 0.0)
        if live == 0:
            rims_hold, grad_out = lax.optimization_barrier((rims_hold, grad_out))
            held_next, held_prev = halo_within(rims_hold, list(range(1, sections)))
        grad_own, grad_prev, grad_next, *grads = pulls[0](grad_out)
        rims = seam_read(jnp.stack([grad_prev, grad_next]), matrices)
        grad_totals = tuple(
            jnp.where(live_step, running + term, running) for running, term in zip(grad_totals, grads)
        )
        if live > 0:
            incoming = send_with_rims(grad_own, rims, live, live - 1)
            if live == sections - 1:
                skip_grad = send_with_rims(grad_own, rims, live, 0)
            own_hold = jnp.where(live_step, grad_own, own_hold)
            rims_hold = jnp.where(live_step, rims, rims_hold)
        else:
            early_grad = assemble(own_hold, held_next, held_prev)
            from_next_tile, from_prev_tile = halo_within(rims, [0])
            last_grad = assemble(grad_own, from_next_tile, from_prev_tile)
            input_grads = jnp.where(section_index == 0, last_grad, early_grad)[None]

    partial = pack_rows(grad_totals, slot_capacity_rows, column_total) * grad_scale
    if tiles & (tiles - 1):
        partial = lax.psum(partial, "tile")
    else:
        step = 1
        while step < tiles:
            pairs = [
                (s * tiles + t, s * tiles + (t ^ step)) for s in range(sections) for t in range(tiles)
            ]
            partial = partial + permute(partial, pairs)
            step *= 2
    grad_weight, grad_kernel, grad_shift, grad_gain = unpack_rows(partial, param_shapes)
    return (
        input_grads[None],
        grad_weight[None],
        grad_kernel[None],
        grad_shift[None],
        grad_gain[None],
    )


def solution(mesh):
    in_specs = (
        P("section", None, None, "tile", None),
        P(None, "section", "tile", None),
        P("section", None, None),
        P("section", None, None),
        P("section", None),
        P("section", None),
        P("tile"),
        P("tile", None),
    )
    out_specs = (
        P("section", None, None, "tile", None),
        P("section", None, None),
        P("section", None, None),
        P("section", None),
        P("section", None),
    )
    return jax.shard_map(
        on_device, mesh=mesh, in_specs=in_specs, out_specs=out_specs, check_vma=False
    )
```

```python
import math

import jax
import jax.numpy as jnp
from jax import lax
from jax.sharding import PartitionSpec as P


KERNEL_DILATION = 4
AXES = ("section", "tile")


def depthwise(extended_block, kernel_taps, slot_capacity_rows):
    column_total = extended_block.shape[2]
    columns = lax.iota(jnp.int32, column_total)
    running = jnp.zeros((extended_block.shape[0], slot_capacity_rows, column_total), jnp.float32)
    for column_offset_tap in range(3):
        offset = (column_offset_tap - 1) * KERNEL_DILATION
        moved = jnp.roll(extended_block, -offset, axis=2)
        inside = jnp.logical_and(columns + offset >= 0, columns + offset < column_total)
        moved = jnp.where(inside[None, None, :], moved, 0.0)
        for row_offset_tap in range(3):
            kernel_window = moved[
                :,
                row_offset_tap * KERNEL_DILATION : row_offset_tap * KERNEL_DILATION
                + slot_capacity_rows,
                :,
            ]
            running = (
                running
                + kernel_taps[3 * row_offset_tap + column_offset_tap][:, None, None] * kernel_window
            )
    return running


def section_forward(
    own_block,
    from_prev,
    received_from_next,
    row_total,
    weight_matrix,
    kernel_taps,
    shift_vector,
    gain_vector,
):
    slot_capacity_rows = own_block.shape[1]
    row_keep = (lax.iota(jnp.int32, slot_capacity_rows) < row_total).astype(jnp.float32)[
        None, :, None
    ]
    masked_block = own_block * row_keep
    extended_block = jnp.concatenate([from_prev, masked_block, jnp.zeros_like(from_prev)], axis=1)
    extended_block = lax.dynamic_update_slice(
        extended_block,
        received_from_next,
        (jnp.int32(0), row_total + KERNEL_DILATION, jnp.int32(0)),
    )
    activation = (
        depthwise(extended_block, kernel_taps, slot_capacity_rows) + shift_vector[:, None, None]
    )
    channel_mean = jnp.mean(activation, axis=0, keepdims=True)
    centered = activation - channel_mean
    variance = jnp.mean(centered * centered, axis=0, keepdims=True)
    normalized = centered * lax.rsqrt(variance + 1e-06) * gain_vector[:, None, None]
    hidden = jax.nn.gelu(normalized)
    mixing = jnp.einsum("oc,crw->orw", weight_matrix, hidden, precision=lax.Precision.HIGHEST)
    return (masked_block + mixing) * row_keep


def permute(x, pairs):
    return lax.ppermute(x, AXES, pairs)


def pack_rows(pieces, slot_rows, column_total):
    flat = jnp.concatenate([piece.reshape(-1) for piece in pieces])
    slab = slot_rows * column_total
    flat = jnp.pad(flat, (0, (-flat.shape[0]) % slab))
    return flat.reshape(-1, slot_rows, column_total)


def unpack_rows(slabs, shapes):
    flat = slabs.reshape(-1)
    out = []
    start = 0
    for shape in shapes:
        size = math.prod(shape)
        out.append(flat[start : start + size].reshape(shape))
        start += size
    return out


def seam_matrices(codes, column_total):
    columns = lax.iota(jnp.int32, column_total)
    plain = (columns[:, None] == columns[None, :]).astype(jnp.float32)
    mirror = (columns[:, None] + columns[None, :] == column_total - 1).astype(jnp.float32)
    return jnp.where((codes == 1)[:, None, None], mirror[None], plain[None])


def seam_read(rims, matrices):
    return jnp.einsum("kcrw,kwv->kcrv", rims, matrices, precision=lax.Precision.HIGHEST)


def edge_rows(own_block, row_total, matrices, pairs_of):
    slot_capacity_rows = own_block.shape[1]
    row_keep = (lax.iota(jnp.int32, slot_capacity_rows) < row_total).astype(jnp.float32)[
        None, :, None
    ]
    masked_block = own_block * row_keep
    leading_rows = masked_block[:, :KERNEL_DILATION, :]
    trailing_rows = lax.dynamic_slice_in_dim(
        masked_block, row_total - KERNEL_DILATION, KERNEL_DILATION, 1
    )
    forward_pairs, backward_pairs = pairs_of
    rims = jnp.stack([permute(trailing_rows, forward_pairs), permute(leading_rows, backward_pairs)])
    rims = seam_read(rims, matrices)
    return rims[0], rims[1]


def on_device(saved_inputs, out_grad, pointwise, kernels, shifts, gains, rows_per_tile, seam_codes):
    sections = lax.axis_size("section")
    tiles = lax.axis_size("tile")
    section_index = lax.axis_index("section")
    row_total = rows_per_tile[0]
    codes = seam_codes[0]
    micro_count = saved_inputs.shape[1]
    channels = saved_inputs.shape[2]
    slot_capacity_rows = saved_inputs.shape[3]
    column_total = saved_inputs.shape[4]
    grad_scale = 1.0 / math.sqrt(micro_count * slot_capacity_rows * tiles * column_total)
    every_section = (
        [(s * tiles + t, s * tiles + (t + 1) % tiles) for s in range(sections) for t in range(tiles)],
        [(s * tiles + (t + 1) % tiles, s * tiles + t) for s in range(sections) for t in range(tiles)],
    )
    params = (pointwise[0], kernels[0], shifts[0], gains[0])
    param_shapes = [pointwise.shape[1:], kernels.shape[1:], shifts.shape[1:], gains.shape[1:]]
    whole_top = lax.all_gather(out_grad, "section", axis=1, tiled=True)
    matrices = seam_matrices(codes, column_total)

    def apply_block(block_in, prev_in, next_in, weight_in, kernel_in, shift_in, gain_in):
        return section_forward(
            block_in, prev_in, next_in, row_total, weight_in, kernel_in, shift_in, gain_in
        )

    pulls = []
    for micro_index in range(micro_count):
        own_block = saved_inputs[0, micro_index]
        from_prev, received_from_next = edge_rows(
            own_block, row_total, matrices, every_section
        )
        _, pull = jax.vjp(apply_block, own_block, from_prev, received_from_next, *params)
        pulls.append(pull)

    def pull_at(slot_index, cotangent):
        if micro_count == 1:
            return pulls[0](cotangent)
        outs = [pull(cotangent) for pull in pulls]
        return tuple(
            sum(jnp.where(slot_index == m, o[k], 0.0) for m, o in enumerate(outs))
            for k in range(len(outs[0]))
        )

    forward_pairs, backward_pairs = every_section

    def assemble(grad_own, from_next_tile, from_prev_tile):
        upper_part = lax.dynamic_update_slice_in_dim(
            jnp.zeros_like(grad_own), from_next_tile, row_total - KERNEL_DILATION, 1
        )
        lower_part = jnp.pad(
            from_prev_tile, ((0, 0), (0, slot_capacity_rows - KERNEL_DILATION), (0, 0))
        )
        return grad_own + upper_part + lower_part

    incoming = jnp.zeros((channels, slot_capacity_rows, column_total), jnp.float32)
    skip_store = jnp.zeros((micro_count, channels, slot_capacity_rows, column_total), jnp.float32)
    input_grads = jnp.zeros((micro_count, channels, slot_capacity_rows, column_total), jnp.float32)
    grad_totals = tuple(jnp.zeros(shape, jnp.float32) for shape in param_shapes)
    step_total = micro_count + sections - 1
    is_last = section_index == sections - 1
    for step_number in range(step_total):
        position = step_number - (sections - 1 - section_index)
        live_step = jnp.logical_and(position >= 0, position < micro_count)
        slot_index = jnp.clip(position, 0, micro_count - 1)
        top_grad = lax.dynamic_index_in_dim(whole_top, slot_index, 0, keepdims=False)
        grad_out = jnp.where(is_last, top_grad, incoming)
        if step_number >= sections - 1:
            carried = lax.dynamic_index_in_dim(skip_store, slot_index, 0, keepdims=False)
            grad_out = grad_out + jnp.where(section_index == 0, carried, 0.0)
        grad_own, grad_prev, grad_next, *grads = pull_at(slot_index, grad_out)
        rims = jnp.stack([grad_prev, grad_next])
        rims = seam_read(rims, matrices)
        live_sections = [
            s for s in range(sections) if 0 <= step_number - (sections - 1 - s) < micro_count
        ]
        if step_number + 1 < step_total:
            senders = [s for s in live_sections if s >= 1]
            next_own = permute(
                grad_own,
                [(s * tiles + t, (s - 1) * tiles + t) for s in senders for t in range(tiles)],
            )
            next_upper = permute(
                rims[0],
                [
                    (s * tiles + (t + 1) % tiles, (s - 1) * tiles + t)
                    for s in senders
                    for t in range(tiles)
                ],
            )
            next_lower = permute(
                rims[1],
                [
                    (s * tiles + t, (s - 1) * tiles + (t + 1) % tiles)
                    for s in senders
                    for t in range(tiles)
                ],
            )
        live_forward = [(a, b) for a, b in forward_pairs if a // tiles in live_sections]
        live_backward = [(a, b) for a, b in backward_pairs if a // tiles in live_sections]
        from_next_tile = permute(rims[0], live_backward)
        from_prev_tile = permute(rims[1], live_forward)
        input_grad = assemble(grad_own, from_next_tile, from_prev_tile)
        grad_totals = tuple(
            jnp.where(live_step, running + term, running) for running, term in zip(grad_totals, grads)
        )
        input_grads = jnp.where(
            live_step,
            lax.dynamic_update_index_in_dim(input_grads, input_grad, slot_index, 0),
            input_grads,
        )
        if step_number + 1 < step_total:
            incoming = assemble(next_own, next_upper, next_lower)
        if step_number == micro_count - 1:
            skip_store = from_behind(input_grads, "section", 1 - sections)

    partial = pack_rows(grad_totals, slot_capacity_rows, column_total) * grad_scale
    if tiles & (tiles - 1):
        partial = lax.psum(partial, "tile")
    else:
        step = 1
        while step < tiles:
            pairs = [
                (s * tiles + t, s * tiles + (t ^ step))
                for s in range(sections)
                for t in range(tiles)
            ]
            partial = partial + permute(partial, pairs)
            step *= 2
    grad_weight, grad_kernel, grad_shift, grad_gain = unpack_rows(partial, param_shapes)
    return (
        input_grads[None],
        grad_weight[None],
        grad_kernel[None],
        grad_shift[None],
        grad_gain[None],
    )


def from_behind(block, axis, distance):
    devices = range(lax.axis_size(axis))
    route = [(i - distance, i) for i in devices if i - distance in devices]
    return lax.ppermute(block, axis, route)


def solution(mesh):
    in_specs = (
        P("section", None, None, "tile", None),
        P(None, "section", "tile", None),
        P("section", None, None),
        P("section", None, None),
        P("section", None),
        P("section", None),
        P("tile"),
        P("tile", None),
    )
    out_specs = (
        P("section", None, None, "tile", None),
        P("section", None, None),
        P("section", None, None),
        P("section", None),
        P("section", None),
    )
    return jax.shard_map(
        on_device, mesh=mesh, in_specs=in_specs, out_specs=out_specs, check_vma=False
    )
```

```python
import math

import jax
import jax.numpy as jnp
from jax import lax
from jax.sharding import PartitionSpec as P


KERNEL_DILATION = 4
AXES = ("section", "tile")


def depthwise(extended_block, kernel_taps, slot_capacity_rows):
    column_total = extended_block.shape[2]
    columns = lax.iota(jnp.int32, column_total)
    running = jnp.zeros((extended_block.shape[0], slot_capacity_rows, column_total), jnp.float32)
    for column_offset_tap in range(3):
        offset = (column_offset_tap - 1) * KERNEL_DILATION
        moved = jnp.roll(extended_block, -offset, axis=2)
        inside = jnp.logical_and(columns + offset >= 0, columns + offset < column_total)
        moved = jnp.where(inside[None, None, :], moved, 0.0)
        for row_offset_tap in range(3):
            kernel_window = moved[
                :,
                row_offset_tap * KERNEL_DILATION : row_offset_tap * KERNEL_DILATION
                + slot_capacity_rows,
                :,
            ]
            running = (
                running
                + kernel_taps[3 * row_offset_tap + column_offset_tap][:, None, None] * kernel_window
            )
    return running


def section_forward(
    own_block,
    from_prev,
    received_from_next,
    row_total,
    weight_matrix,
    kernel_taps,
    shift_vector,
    gain_vector,
):
    slot_capacity_rows = own_block.shape[1]
    row_keep = (lax.iota(jnp.int32, slot_capacity_rows) < row_total).astype(jnp.float32)[
        None, :, None
    ]
    masked_block = own_block * row_keep
    extended_block = jnp.concatenate([from_prev, masked_block, jnp.zeros_like(from_prev)], axis=1)
    extended_block = lax.dynamic_update_slice(
        extended_block,
        received_from_next,
        (jnp.int32(0), row_total + KERNEL_DILATION, jnp.int32(0)),
    )
    activation = (
        depthwise(extended_block, kernel_taps, slot_capacity_rows) + shift_vector[:, None, None]
    )
    channel_mean = jnp.mean(activation, axis=0, keepdims=True)
    centered = activation - channel_mean
    variance = jnp.mean(centered * centered, axis=0, keepdims=True)
    normalized = centered * lax.rsqrt(variance + 1e-06) * gain_vector[:, None, None]
    hidden = jax.nn.gelu(normalized)
    mixing = jnp.einsum("oc,crw->orw", weight_matrix, hidden, precision=lax.Precision.HIGHEST)
    return (masked_block + mixing) * row_keep


def permute(x, pairs):
    return lax.ppermute(x, AXES, pairs)


def seam_matrices(codes, column_total):
    columns = lax.iota(jnp.int32, column_total)
    plain = (columns[:, None] == columns[None, :]).astype(jnp.float32)
    mirror = (columns[:, None] + columns[None, :] == column_total - 1).astype(jnp.float32)
    return jnp.where((codes == 1)[:, None, None], mirror[None], plain[None])


def seam_read(rims, matrices):
    return jnp.einsum("kcrw,kwv->kcrv", rims, matrices, precision=lax.Precision.HIGHEST)


def edge_rows(own_block, row_total, matrices, pairs_of):
    slot_capacity_rows = own_block.shape[1]
    row_keep = (lax.iota(jnp.int32, slot_capacity_rows) < row_total).astype(jnp.float32)[
        None, :, None
    ]
    masked_block = own_block * row_keep
    leading_rows = masked_block[:, :KERNEL_DILATION, :]
    trailing_rows = lax.dynamic_slice_in_dim(
        masked_block, row_total - KERNEL_DILATION, KERNEL_DILATION, 1
    )
    forward_pairs, backward_pairs = pairs_of
    rims = jnp.stack([permute(trailing_rows, forward_pairs), permute(leading_rows, backward_pairs)])
    rims = seam_read(rims, matrices)
    return rims[0], rims[1]


def on_device(saved_inputs, out_grad, pointwise, kernels, shifts, gains, rows_per_tile, seam_codes):
    sections = lax.axis_size("section")
    tiles = lax.axis_size("tile")
    section_index = lax.axis_index("section")
    row_total = rows_per_tile[0]
    codes = seam_codes[0]
    micro_count = saved_inputs.shape[1]
    channels = saved_inputs.shape[2]
    slot_capacity_rows = saved_inputs.shape[3]
    column_total = saved_inputs.shape[4]
    grad_scale = 1.0 / math.sqrt(micro_count * slot_capacity_rows * tiles * column_total)
    every_section = (
        [(s * tiles + t, s * tiles + (t + 1) % tiles) for s in range(sections) for t in range(tiles)],
        [(s * tiles + (t + 1) % tiles, s * tiles + t) for s in range(sections) for t in range(tiles)],
    )
    params = (pointwise[0], kernels[0], shifts[0], gains[0])
    param_shapes = [pointwise.shape[1:], kernels.shape[1:], shifts.shape[1:], gains.shape[1:]]
    whole_top = lax.all_gather(out_grad, "section", axis=1, tiled=True)
    matrices = seam_matrices(codes, column_total)

    def apply_block(block_in, prev_in, next_in, weight_in, kernel_in, shift_in, gain_in):
        return section_forward(
            block_in, prev_in, next_in, row_total, weight_in, kernel_in, shift_in, gain_in
        )

    pulls = []
    for micro_index in range(micro_count):
        own_block = saved_inputs[0, micro_index]
        from_prev, received_from_next = edge_rows(
            own_block, row_total, matrices, every_section
        )
        _, pull = jax.vjp(apply_block, own_block, from_prev, received_from_next, *params)
        pulls.append(pull)

    def pull_at(slot_index, cotangent):
        if micro_count == 1:
            return pulls[0](cotangent)
        outs = [pull(cotangent) for pull in pulls]
        return tuple(
            sum(jnp.where(slot_index == m, o[k], 0.0) for m, o in enumerate(outs))
            for k in range(len(outs[0]))
        )

    forward_pairs, backward_pairs = every_section

    def assemble(grad_own, from_next_tile, from_prev_tile):
        upper_part = lax.dynamic_update_slice_in_dim(
            jnp.zeros_like(grad_own), from_next_tile, row_total - KERNEL_DILATION, 1
        )
        lower_part = jnp.pad(
            from_prev_tile, ((0, 0), (0, slot_capacity_rows - KERNEL_DILATION), (0, 0))
        )
        return grad_own + upper_part + lower_part

    incoming = jnp.zeros((channels, slot_capacity_rows, column_total), jnp.float32)
    skip_store = jnp.zeros((micro_count, channels, slot_capacity_rows, column_total), jnp.float32)
    input_grads = jnp.zeros((micro_count, channels, slot_capacity_rows, column_total), jnp.float32)
    grad_totals = tuple(jnp.zeros(shape, jnp.float32) for shape in param_shapes)
    step_total = micro_count + sections - 1
    is_last = section_index == sections - 1
    for step_number in range(step_total):
        position = step_number - (sections - 1 - section_index)
        live_step = jnp.logical_and(position >= 0, position < micro_count)
        slot_index = jnp.clip(position, 0, micro_count - 1)
        top_grad = lax.dynamic_index_in_dim(whole_top, slot_index, 0, keepdims=False)
        grad_out = jnp.where(is_last, top_grad, incoming)
        if step_number >= sections - 1:
            carried = lax.dynamic_index_in_dim(skip_store, slot_index, 0, keepdims=False)
            grad_out = grad_out + jnp.where(section_index == 0, carried, 0.0)
        grad_own, grad_prev, grad_next, *grads = pull_at(slot_index, grad_out)
        rims = jnp.stack([grad_prev, grad_next])
        rims = seam_read(rims, matrices)
        live_sections = [
            s for s in range(sections) if 0 <= step_number - (sections - 1 - s) < micro_count
        ]
        if step_number + 1 < step_total:
            senders = [s for s in live_sections if s >= 1]
            next_own = permute(
                grad_own,
                [(s * tiles + t, (s - 1) * tiles + t) for s in senders for t in range(tiles)],
            )
            next_upper = permute(
                rims[0],
                [
                    (s * tiles + (t + 1) % tiles, (s - 1) * tiles + t)
                    for s in senders
                    for t in range(tiles)
                ],
            )
            next_lower = permute(
                rims[1],
                [
                    (s * tiles + t, (s - 1) * tiles + (t + 1) % tiles)
                    for s in senders
                    for t in range(tiles)
                ],
            )
        live_forward = [(a, b) for a, b in forward_pairs if a // tiles in live_sections]
        live_backward = [(a, b) for a, b in backward_pairs if a // tiles in live_sections]
        from_next_tile = permute(rims[0], live_backward)
        from_prev_tile = permute(rims[1], live_forward)
        input_grad = assemble(grad_own, from_next_tile, from_prev_tile)
        grad_totals = tuple(
            jnp.where(live_step, running + term, running) for running, term in zip(grad_totals, grads)
        )
        input_grads = jnp.where(
            live_step,
            lax.dynamic_update_index_in_dim(input_grads, input_grad, slot_index, 0),
            input_grads,
        )
        if step_number + 1 < step_total:
            incoming = assemble(next_own, next_upper, next_lower)
        if step_number == micro_count - 1:
            skip_store = from_behind(input_grads, "section", 1 - sections)

    rows = jnp.concatenate(
        [grad_totals[0], grad_totals[1], grad_totals[2][None], grad_totals[3][None]], axis=0
    )
    partial = jnp.pad(rows, ((0, (-rows.shape[0]) % 8), (0, 0))) * grad_scale
    if tiles & (tiles - 1):
        partial = lax.psum(partial, "tile")
    else:
        step = 1
        while step < tiles:
            pairs = [
                (s * tiles + t, s * tiles + (t ^ step)) for s in range(sections) for t in range(tiles)
            ]
            partial = partial + permute(partial, pairs)
            step *= 2
    kernel_rows = param_shapes[1][0]
    grad_weight = partial[:channels]
    grad_kernel = partial[channels : channels + kernel_rows]
    grad_shift = partial[channels + kernel_rows]
    grad_gain = partial[channels + kernel_rows + 1]
    return (
        input_grads[None],
        grad_weight[None],
        grad_kernel[None],
        grad_shift[None],
        grad_gain[None],
    )


def from_behind(block, axis, distance):
    devices = range(lax.axis_size(axis))
    route = [(i - distance, i) for i in devices if i - distance in devices]
    return lax.ppermute(block, axis, route)


def solution(mesh):
    in_specs = (
        P("section", None, None, "tile", None),
        P(None, "section", "tile", None),
        P("section", None, None),
        P("section", None, None),
        P("section", None),
        P("section", None),
        P("tile"),
        P("tile", None),
    )
    out_specs = (
        P("section", None, None, "tile", None),
        P("section", None, None),
        P("section", None, None),
        P("section", None),
        P("section", None),
    )
    return jax.shard_map(
        on_device, mesh=mesh, in_specs=in_specs, out_specs=out_specs, check_vma=False
    )
```

```python
import math

import jax
import jax.numpy as jnp
from jax import lax
from jax.sharding import PartitionSpec as P


KERNEL_DILATION = 4
AXES = ("section", "tile")


def depthwise(extended_block, kernel_taps, slot_capacity_rows):
    column_total = extended_block.shape[2]
    columns = lax.iota(jnp.int32, column_total)
    running = jnp.zeros((extended_block.shape[0], slot_capacity_rows, column_total), jnp.float32)
    for column_offset_tap in range(3):
        offset = (column_offset_tap - 1) * KERNEL_DILATION
        moved = jnp.roll(extended_block, -offset, axis=2)
        inside = jnp.logical_and(columns + offset >= 0, columns + offset < column_total)
        moved = jnp.where(inside[None, None, :], moved, 0.0)
        for row_offset_tap in range(3):
            kernel_window = moved[
                :,
                row_offset_tap * KERNEL_DILATION : row_offset_tap * KERNEL_DILATION
                + slot_capacity_rows,
                :,
            ]
            running = (
                running
                + kernel_taps[3 * row_offset_tap + column_offset_tap][:, None, None] * kernel_window
            )
    return running


def section_forward(
    own_block,
    from_prev,
    received_from_next,
    row_total,
    weight_matrix,
    kernel_taps,
    shift_vector,
    gain_vector,
):
    slot_capacity_rows = own_block.shape[1]
    row_keep = (lax.iota(jnp.int32, slot_capacity_rows) < row_total).astype(jnp.float32)[
        None, :, None
    ]
    masked_block = own_block * row_keep
    extended_block = jnp.concatenate([from_prev, masked_block, jnp.zeros_like(from_prev)], axis=1)
    extended_block = lax.dynamic_update_slice(
        extended_block,
        received_from_next,
        (jnp.int32(0), row_total + KERNEL_DILATION, jnp.int32(0)),
    )
    activation = (
        depthwise(extended_block, kernel_taps, slot_capacity_rows) + shift_vector[:, None, None]
    )
    channel_mean = jnp.mean(activation, axis=0, keepdims=True)
    centered = activation - channel_mean
    variance = jnp.mean(centered * centered, axis=0, keepdims=True)
    normalized = centered * lax.rsqrt(variance + 1e-06) * gain_vector[:, None, None]
    hidden = jax.nn.gelu(normalized)
    mixing = jnp.einsum("oc,crw->orw", weight_matrix, hidden, precision=lax.Precision.HIGHEST)
    return (masked_block + mixing) * row_keep


def permute(x, pairs):
    return lax.ppermute(x, AXES, pairs)


def seam_matrices(codes, column_total):
    columns = lax.iota(jnp.int32, column_total)
    plain = (columns[:, None] == columns[None, :]).astype(jnp.float32)
    mirror = (columns[:, None] + columns[None, :] == column_total - 1).astype(jnp.float32)
    return jnp.where((codes == 1)[:, None, None], mirror[None], plain[None])


def seam_read(rims, matrices):
    return jnp.einsum("kcrw,kwv->kcrv", rims, matrices, precision=lax.Precision.HIGHEST)


def edge_rows(own_block, row_total, matrices, pairs_of):
    slot_capacity_rows = own_block.shape[1]
    row_keep = (lax.iota(jnp.int32, slot_capacity_rows) < row_total).astype(jnp.float32)[
        None, :, None
    ]
    masked_block = own_block * row_keep
    leading_rows = masked_block[:, :KERNEL_DILATION, :]
    trailing_rows = lax.dynamic_slice_in_dim(
        masked_block, row_total - KERNEL_DILATION, KERNEL_DILATION, 1
    )
    forward_pairs, backward_pairs = pairs_of
    rims = jnp.stack([permute(trailing_rows, forward_pairs), permute(leading_rows, backward_pairs)])
    rims = seam_read(rims, matrices)
    return rims[0], rims[1]


def on_device(saved_inputs, out_grad, pointwise, kernels, shifts, gains, rows_per_tile, seam_codes):
    sections = lax.axis_size("section")
    tiles = lax.axis_size("tile")
    section_index = lax.axis_index("section")
    row_total = rows_per_tile[0]
    codes = seam_codes[0]
    micro_count = saved_inputs.shape[1]
    channels = saved_inputs.shape[2]
    slot_capacity_rows = saved_inputs.shape[3]
    column_total = saved_inputs.shape[4]
    grad_scale = 1.0 / math.sqrt(micro_count * slot_capacity_rows * tiles * column_total)
    every_section = (
        [(s * tiles + t, s * tiles + (t + 1) % tiles) for s in range(sections) for t in range(tiles)],
        [(s * tiles + (t + 1) % tiles, s * tiles + t) for s in range(sections) for t in range(tiles)],
    )
    params = (pointwise[0], kernels[0], shifts[0], gains[0])
    param_shapes = [pointwise.shape[1:], kernels.shape[1:], shifts.shape[1:], gains.shape[1:]]
    whole_top = lax.all_gather(out_grad, "section", axis=1, tiled=True)
    matrices = seam_matrices(codes, column_total)

    def apply_block(block_in, prev_in, next_in, weight_in, kernel_in, shift_in, gain_in):
        return section_forward(
            block_in, prev_in, next_in, row_total, weight_in, kernel_in, shift_in, gain_in
        )

    pulls = []
    for micro_index in range(micro_count):
        own_block = saved_inputs[0, micro_index]
        from_prev, received_from_next = edge_rows(
            own_block, row_total, matrices, every_section
        )
        _, pull = jax.vjp(apply_block, own_block, from_prev, received_from_next, *params)
        pulls.append(pull)

    def pull_at(slot_index, cotangent):
        if micro_count == 1:
            return pulls[0](cotangent)
        outs = [pull(cotangent) for pull in pulls]
        return tuple(
            sum(jnp.where(slot_index == m, o[k], 0.0) for m, o in enumerate(outs))
            for k in range(len(outs[0]))
        )

    forward_pairs, backward_pairs = every_section

    def assemble(grad_own, from_next_tile, from_prev_tile):
        upper_part = lax.dynamic_update_slice_in_dim(
            jnp.zeros_like(grad_own), from_next_tile, row_total - KERNEL_DILATION, 1
        )
        lower_part = jnp.pad(
            from_prev_tile, ((0, 0), (0, slot_capacity_rows - KERNEL_DILATION), (0, 0))
        )
        return grad_own + upper_part + lower_part

    incoming = jnp.zeros((channels, slot_capacity_rows, column_total), jnp.float32)
    skip_store = jnp.zeros((micro_count, channels, slot_capacity_rows, column_total), jnp.float32)
    input_grads = jnp.zeros((micro_count, channels, slot_capacity_rows, column_total), jnp.float32)
    grad_totals = tuple(jnp.zeros(shape, jnp.float32) for shape in param_shapes)
    step_total = micro_count + sections - 1
    is_last = section_index == sections - 1
    for step_number in range(step_total):
        position = step_number - (sections - 1 - section_index)
        live_step = jnp.logical_and(position >= 0, position < micro_count)
        slot_index = jnp.clip(position, 0, micro_count - 1)
        top_grad = lax.dynamic_index_in_dim(whole_top, slot_index, 0, keepdims=False)
        grad_out = jnp.where(is_last, top_grad, incoming)
        if step_number >= sections - 1:
            carried = lax.dynamic_index_in_dim(skip_store, slot_index, 0, keepdims=False)
            grad_out = grad_out + jnp.where(section_index == 0, carried, 0.0)
        grad_own, grad_prev, grad_next, *grads = pull_at(slot_index, grad_out)
        rims = jnp.stack([grad_prev, grad_next])
        rims = seam_read(rims, matrices)
        live_sections = [
            s for s in range(sections) if 0 <= step_number - (sections - 1 - s) < micro_count
        ]
        if step_number + 1 < step_total:
            senders = [s for s in live_sections if s >= 1]
            next_own = permute(
                grad_own,
                [(s * tiles + t, (s - 1) * tiles + t) for s in senders for t in range(tiles)],
            )
            next_upper = permute(
                rims[0],
                [
                    (s * tiles + (t + 1) % tiles, (s - 1) * tiles + t)
                    for s in senders
                    for t in range(tiles)
                ],
            )
            next_lower = permute(
                rims[1],
                [
                    (s * tiles + t, (s - 1) * tiles + (t + 1) % tiles)
                    for s in senders
                    for t in range(tiles)
                ],
            )
        live_forward = [(a, b) for a, b in forward_pairs if a // tiles in live_sections]
        live_backward = [(a, b) for a, b in backward_pairs if a // tiles in live_sections]
        from_next_tile = permute(rims[0], live_backward)
        from_prev_tile = permute(rims[1], live_forward)
        input_grad = assemble(grad_own, from_next_tile, from_prev_tile)
        grad_totals = tuple(
            jnp.where(live_step, running + term, running) for running, term in zip(grad_totals, grads)
        )
        input_grads = jnp.where(
            live_step,
            lax.dynamic_update_index_in_dim(input_grads, input_grad, slot_index, 0),
            input_grads,
        )
        if step_number + 1 < step_total:
            incoming = assemble(next_own, next_upper, next_lower)
        if step_number == micro_count - 1:
            skip_store = from_behind(input_grads, "section", 1 - sections)

    rows = jnp.concatenate(
        [grad_totals[0], grad_totals[1], grad_totals[2][None], grad_totals[3][None]], axis=0
    )
    partial = jnp.pad(rows, ((0, (-rows.shape[0]) % 8), (0, 0))) * grad_scale
    if tiles & (tiles - 1):
        partial = lax.psum(partial, "tile")
    else:
        step = tiles // 2
        while step >= 1:
            pairs = [
                (s * tiles + t, s * tiles + (t ^ step)) for s in range(sections) for t in range(tiles)
            ]
            partial = partial + permute(partial, pairs)
            step //= 2
    kernel_rows = param_shapes[1][0]
    grad_weight = partial[:channels]
    grad_kernel = partial[channels : channels + kernel_rows]
    grad_shift = partial[channels + kernel_rows]
    grad_gain = partial[channels + kernel_rows + 1]
    return (
        input_grads[None],
        grad_weight[None],
        grad_kernel[None],
        grad_shift[None],
        grad_gain[None],
    )


def from_behind(block, axis, distance):
    devices = range(lax.axis_size(axis))
    route = [(i - distance, i) for i in devices if i - distance in devices]
    return lax.ppermute(block, axis, route)


def solution(mesh):
    in_specs = (
        P("section", None, None, "tile", None),
        P(None, "section", "tile", None),
        P("section", None, None),
        P("section", None, None),
        P("section", None),
        P("section", None),
        P("tile"),
        P("tile", None),
    )
    out_specs = (
        P("section", None, None, "tile", None),
        P("section", None, None),
        P("section", None, None),
        P("section", None),
        P("section", None),
    )
    return jax.shard_map(
        on_device, mesh=mesh, in_specs=in_specs, out_specs=out_specs, check_vma=False
    )
```
